32 devices in a mesh: case: 2 (over y), tm: 4 (over z), bundle: 2 (over x), sub: 2 (over core).
Axes of the slice: x: 2, y: 2, z: 4, core: 2. Of those that a mesh axis runs over, the one named last changes fastest.
Arguments:
- cotangent: bfloat16 [16384, 512], P(('case', 'tm'), 'bundle'), parts along dimension 0, may hold values from -28 to 28
- inputs: bfloat16 [16384, 512], P(('case', 'tm'), 'bundle'), parts along dimension 0, may hold values from -6 to 6
- impulse: bfloat16 [8, 128, 4096], P('bundle', 'sub'), may hold values from -0.0625 to 0.0625
- terminal: int32 [8, 64], P('bundle'), may hold values from 0 to 63, each once within a row
- fault_step: int32 [2], P('case'), parts along dimension 0, may hold values from 0 to 4095
Outputs:
- voltage_grad: bfloat16 [16384, 512], P(('case', 'tm', 'sub'), 'bundle'), parts along dimension 0
- impulse_grad: float32 [16, 128, 4096], P(('case', 'bundle'), 'sub', 'tm'), parts along dimension 0
The draws below stay inside these ranges and needn't reach their ends.
There are 2 independent parts, one for each index of `case`. The reference program is written for one: setup_inputs(seed, part) draws one part's arguments, and reference() takes and returns one part's arrays. A program takes and returns all parts, laid end to end along the dimension named above; an argument that names none is the same for every part. Nothing has to cross between parts.
Inputs may be any that keep to these rules, and one draw needn't show every extreme that they name: Each row of terminal orders the 64 terminals of a bundle, each once.
All inputs are finite; a program needn't handle non-finite values.
Results may differ from the reference program's by a relative error of at most 0.001.
Values may be sent and summed in bfloat16 or wider, within the bound.
No kernel may reach another device: no remote copies, remote signals or barrier semaphores. Data moves between devices by JAX's collectives and lax.ppermute only.
A program may use at most 320 MiB of HBM per device.

```python
import jax
import jax.numpy as jnp
from jax import lax

CB = 64
NB = 8
L = 128
TOTAL = 8192


def draw_cotangent(key, part):
    first_key, second_key = jax.random.split(key, 2)
    steps_all = jnp.arange(TOTAL, dtype=jnp.float32)
    ramp = 3.0 ** (steps_all / (TOTAL - 1) - 0.5)
    spread = jax.random.uniform(second_key, (NB * CB,), jnp.float32) - 0.5
    base_vals = jax.random.truncated_normal(first_key, -4.0, 4.0, (TOTAL, NB * CB), jnp.float32)
    scales = 10.0 ** spread
    return (base_vals * ramp[:, None] * scales[None, :]).astype(jnp.bfloat16)


def block_scale(key, extent, pieces, least, top_value):
    gain = 1.0
    for position, parts in pieces:
        draws = jax.random.uniform(jax.random.fold_in(jax.random.fold_in(key, 6), position), (parts,), jnp.float32, least / len(pieces), top_value / len(pieces))
        gain = gain * jnp.repeat(jnp.exp(draws), extent[position] // parts).reshape((-1,) + (1,) * (len(extent) - 1 - position))
    return gain


def bell_draw(stream_key, shape, scale, most, cuts=(), held_as=jnp.bfloat16):
    level = block_scale(stream_key, shape, cuts, -0.22, 0.18) if cuts else 1.0
    result = jax.random.normal(stream_key, shape, jnp.float32) * scale * level
    return jnp.minimum(jnp.maximum(result, -most), most).astype(held_as)


def setup_inputs(seed: int = 0, part: int = 0) -> dict:
    splits = jax.random.split(jax.random.key(seed), 6)
    part_keys = jax.random.split(jax.random.fold_in(splits[5], part), 6)
    cotangent = draw_cotangent(jax.random.fold_in(jax.random.fold_in(splits[5], part), 71), part)
    inputs = bell_draw(part_keys[1], (TOTAL, NB * CB), 1.0, 6.0, ((0, 4), (1, 2)))
    impulse = bell_draw(splits[2], (NB, L, CB * CB), (L * CB) ** -0.5, 0.0625, ((0, 2), (1, 2)))
    terminal = jax.vmap(lambda own: jax.random.permutation(own, CB))(jax.random.split(splits[3], NB)).reshape((NB, CB)).astype(jnp.int32)
    fault_step = jax.random.randint(part_keys[4], (1,), 0, TOTAL // 2).astype(jnp.int32)
    return {"cotangent": cotangent, "inputs": inputs, "impulse": impulse, "terminal": terminal, "fault_step": fault_step}


norm_ratio = 0.5

def reference(cotangent, inputs, impulse, terminal, fault_step):
    times = jnp.arange(TOTAL, dtype=jnp.int32)
    live = (times >= fault_step[0]).astype(jnp.float32)
    block_rows = min(512, TOTAL)
    block_count = TOTAL // block_rows
    columns = jnp.arange(CB, dtype=jnp.int32)
    dx_parts = []
    grad_parts = []
    for bundle_index in range(NB):
        grad_cols = cotangent[:, bundle_index * CB:(bundle_index + 1) * CB]
        onehot = (terminal[bundle_index][:, None] == columns[None, :]).astype(jnp.bfloat16)
        reordered = jnp.dot(grad_cols, onehot, preferred_element_type=jnp.float32).astype(jnp.bfloat16)
        volt_cols = inputs[:, bundle_index * CB:(bundle_index + 1) * CB]
        masked = (volt_cols.astype(jnp.float32) * live[:, None]).astype(jnp.bfloat16)
        padded = jnp.concatenate([reordered, jnp.zeros((L, CB), jnp.bfloat16)], axis=0)
        kernel = impulse[bundle_index].reshape(L, CB, CB).astype(jnp.float32)

        def advance(grad_acc, block_index):
            row_start = (block_index * block_rows).astype(jnp.int32)
            window = lax.dynamic_slice_in_dim(padded, row_start, block_rows + L, 0).astype(jnp.float32)
            unfolded = jnp.stack([window[shift_lag:shift_lag + block_rows] for shift_lag in range(L)], axis=1)
            row_block = lax.dynamic_slice_in_dim(masked, row_start, block_rows, 0).astype(jnp.float32)
            dx_block = jnp.einsum('tmr,mrj->tj', unfolded, kernel)
            grad_acc = grad_acc + jnp.einsum('tmr,tj->mrj', unfolded, row_block)
            return (grad_acc, dx_block)
        grad_acc, dx_blocks = lax.scan(advance, jnp.zeros((L, CB, CB), jnp.float32), jnp.arange(block_count, dtype=jnp.int32))
        dx_parts.append(dx_blocks.reshape(TOTAL, CB) * live[:, None])
        grad_parts.append(grad_acc.reshape(L, CB * CB))
    voltage_grad = jnp.concatenate(dx_parts, axis=1).astype(jnp.bfloat16)
    raw = jnp.stack(grad_parts, axis=0)
    total_norm = jnp.sqrt(jnp.sum(raw * raw) + 1e-06)
    norm_limit = norm_ratio * (NB * L * CB * CB) ** 0.5
    impulse_grad = raw * (norm_limit / total_norm)
    return (voltage_grad, impulse_grad)
```

```python
import functools
import math

import jax
import jax.numpy as jnp
from jax import lax
from jax.experimental import pallas as pl
from jax.sharding import PartitionSpec as P

CB = 64
NB = 8
L = 128


norm_ratio = 0.5
tile_rows = 4
chunk_rows = 256
_INTERPRET = False


def passed_along(block, axis, distance):
    devices = range(lax.axis_size(axis))
    route = [(i - distance, i) for i in devices if i - distance in devices]
    return lax.ppermute(block, axis, route)


def dx_kernel(r_ref, t_ref, o_ref, *, lag_tiles, rows):
    width = o_ref.shape[2]
    for c in range(rows // chunk_rows):
        base = c * chunk_rows
        acc = jnp.zeros((chunk_rows, width), jnp.float32)
        for q in range(lag_tiles):
            x = r_ref[0, base + q : base + q + chunk_rows, :].astype(jnp.bfloat16)
            acc = acc + jnp.dot(x, t_ref[0, q], preferred_element_type=jnp.float32)
        o_ref[0, base : base + chunk_rows, :] = acc


def raw_kernel(rt_ref, m_ref, o_ref, *, shift, rows, width):
    rt = rt_ref[0]

    def corr(q):
        m = m_ref[0, shift - q : shift - q + rows, :].astype(jnp.bfloat16)
        return jnp.dot(rt, m, preferred_element_type=jnp.float32)

    g_prev = corr(0)
    for a in range(shift):
        g_next = corr(a + 1)
        for d in range(tile_rows):
            acc = None
            for s in range(tile_rows):
                u = s - d
                if 0 <= u < tile_rows:
                    blk = g_prev[s * width : (s + 1) * width, u * width : (u + 1) * width]
                    acc = blk if acc is None else acc + blk
                u = s - d + tile_rows
                if 0 <= u < tile_rows:
                    blk = g_next[s * width : (s + 1) * width, u * width : (u + 1) * width]
                    acc = blk if acc is None else acc + blk
            o_ref[0, tile_rows * a + d] = acc
        g_prev = g_next


def local(cotangent, inputs, impulse, terminal, fault_step):
    seg_rows = cotangent.shape[0]
    nb = terminal.shape[0]
    width = terminal.shape[1]
    lag_count = impulse.shape[1]
    n_sub = lax.axis_size("sub")
    sub = lax.axis_index("sub")
    all_lags = lag_count * n_sub
    tr = tile_rows
    rows4 = seg_rows // tr
    wide = tr * width
    shift = lag_count // tr
    halo = all_lags // tr
    lag_tiles = shift + 1

    columns = jnp.arange(width, dtype=jnp.int32)
    onehot = (terminal[:, :, None] == columns[None, None, :]).astype(jnp.bfloat16)
    cot4 = cotangent.reshape(rows4, tr, nb, width)
    reord4 = jnp.einsum(
        "ksbi,bir->bksr", cot4, onehot, preferred_element_type=jnp.float32
    ).astype(jnp.bfloat16)
    r4 = reord4.reshape(nb, rows4, wide)
    r4t = jnp.transpose(reord4, (0, 2, 3, 1)).reshape(nb, wide, rows4)

    seg_start = lax.axis_index("tm") * seg_rows
    steps4 = seg_start + tr * jnp.arange(rows4, dtype=jnp.int32)[:, None] + jnp.arange(tr, dtype=jnp.int32)[None, :]
    live4 = steps4 >= fault_step[0]
    inp4 = jnp.transpose(inputs.reshape(rows4, tr, nb, width), (2, 0, 1, 3))
    m4 = jnp.where(live4[None, :, :, None], inp4, jnp.zeros((), jnp.bfloat16)).reshape(nb, rows4, wide)

    ahead = passed_along(r4[:, :halo], "tm", -1)
    r4ext = jnp.concatenate([r4, ahead], axis=1).astype(jnp.float32)
    r4w = lax.dynamic_slice_in_dim(r4ext, sub * shift, rows4 + shift, 1)
    behind = passed_along(m4[:, rows4 - halo :], "tm", 1)
    m4ext = jnp.concatenate([behind, m4], axis=1).astype(jnp.float32)
    m4w = lax.dynamic_slice_in_dim(m4ext, (n_sub - 1 - sub) * shift, rows4 + shift, 1)

    kern = impulse.reshape(nb, lag_count, width, width)
    kpad = jnp.pad(kern, ((0, 0), (tr - 1, tr), (0, 0), (0, 0)))
    rows_of = []
    for s in range(tr):
        cols_of = []
        for u in range(tr):
            start = s - u + tr - 1
            cols_of.append(lax.slice_in_dim(kpad, start, start + tr * shift + 1, tr, 1))
        rows_of.append(jnp.stack(cols_of, axis=3))
    toeplitz = jnp.stack(rows_of, axis=2).reshape(nb, lag_tiles, wide, wide)

    partial_dx = pl.pallas_call(
        functools.partial(dx_kernel, lag_tiles=lag_tiles, rows=rows4),
        grid=(nb,),
        in_specs=[
            pl.BlockSpec((1, rows4 + shift, wide), lambda b: (b, 0, 0)),
            pl.BlockSpec((1, lag_tiles, wide, wide), lambda b: (b, 0, 0, 0)),
        ],
        out_specs=pl.BlockSpec((1, rows4, wide), lambda b: (b, 0, 0)),
        out_shape=jax.ShapeDtypeStruct((nb, rows4, wide), jnp.float32),
        interpret=_INTERPRET,
    )(r4w, toeplitz)

    raw = pl.pallas_call(
        functools.partial(raw_kernel, shift=shift, rows=rows4, width=width),
        grid=(nb,),
        in_specs=[
            pl.BlockSpec((1, wide, rows4), lambda b: (b, 0, 0)),
            pl.BlockSpec((1, rows4 + shift, wide), lambda b: (b, 0, 0)),
        ],
        out_specs=pl.BlockSpec((1, lag_count, width, width), lambda b: (b, 0, 0, 0)),
        out_shape=jax.ShapeDtypeStruct((nb, lag_count, width, width), jnp.float32),
        interpret=_INTERPRET,
    )(r4t, m4w)

    summed_dx = lax.psum_scatter(partial_dx, "sub", scatter_dimension=1, tiled=True)
    share4 = summed_dx.shape[1]
    own_steps = (
        seg_start
        + sub * share4 * tr
        + tr * jnp.arange(share4, dtype=jnp.int32)[:, None]
        + jnp.arange(tr, dtype=jnp.int32)[None, :]
    )
    dx = jnp.where(
        (own_steps >= fault_step[0])[None, :, :, None],
        summed_dx.reshape(nb, share4, tr, width),
        0.0,
    ).astype(jnp.bfloat16)
    voltage_grad = jnp.transpose(dx, (1, 2, 0, 3)).reshape(share4 * tr, nb * width)

    grad_flat = raw.reshape(nb, lag_count, width * width)
    own_grad = lax.psum_scatter(grad_flat, "tm", scatter_dimension=2, tiled=True)
    own_squares = jnp.sum(own_grad * own_grad)
    total_squares = lax.psum(own_squares, ("tm", "bundle", "sub"))
    norm_limit = norm_ratio * math.sqrt(NB * L * CB * CB)
    factor = norm_limit / jnp.sqrt(total_squares + 1e-06)
    return (voltage_grad, own_grad * factor)


def solution(mesh):
    placed = (
        P(("case", "tm"), "bundle"),
        P(("case", "tm"), "bundle"),
        P("bundle", "sub", None),
        P("bundle", None),
        P("case"),
    )
    return jax.shard_map(
        local,
        mesh=mesh,
        in_specs=placed,
        out_specs=(P(("case", "tm", "sub"), "bundle"), P(("case", "bundle"), "sub", "tm")),
        check_vma=False,
    )
```

```python
import functools
import math

import jax
import jax.numpy as jnp
from jax import lax
from jax.experimental import pallas as pl
from jax.sharding import PartitionSpec as P

CB = 64
NB = 8
L = 128


norm_ratio = 0.5
tile_rows = 4
chunk_rows = 256
_INTERPRET = False


def passed_along(block, axis, distance):
    devices = range(lax.axis_size(axis))
    route = [(i - distance, i) for i in devices if i - distance in devices]
    return lax.ppermute(block, axis, route)


def dx_kernel(r_ref, t_ref, o_ref, *, lag_tiles, rows):
    width = o_ref.shape[2]
    width_t = t_ref.shape[2]
    for c in range(rows // chunk_rows):
        base = c * chunk_rows
        acc = jnp.zeros((chunk_rows, width), jnp.float32)
        for q in range(lag_tiles):
            x = r_ref[0, base + q : base + q + chunk_rows, :].astype(jnp.bfloat16)
            acc = acc + jnp.dot(x, t_ref[0, q * width_t : (q + 1) * width_t, :], preferred_element_type=jnp.float32)
        o_ref[0, base : base + chunk_rows, :] = acc


def raw_kernel(rt_ref, m_ref, o_ref, *, shift, rows, width):
    rt = rt_ref[0]

    def corr(q):
        m = m_ref[0, shift - q : shift - q + rows, :].astype(jnp.bfloat16)
        return jnp.dot(rt, m, preferred_element_type=jnp.float32)

    g_prev = corr(0)
    for a in range(shift):
        g_next = corr(a + 1)
        for d in range(tile_rows):
            acc = None
            for s in range(tile_rows):
                u = s - d
                if 0 <= u < tile_rows:
                    blk = g_prev[s * width : (s + 1) * width, u * width : (u + 1) * width]
                    acc = blk if acc is None else acc + blk
                u = s - d + tile_rows
                if 0 <= u < tile_rows:
                    blk = g_next[s * width : (s + 1) * width, u * width : (u + 1) * width]
                    acc = blk if acc is None else acc + blk
            o_ref[0, tile_rows * a + d] = acc
        g_prev = g_next


def local(cotangent, inputs, impulse, terminal, fault_step):
    seg_rows = cotangent.shape[0]
    nb = terminal.shape[0]
    width = terminal.shape[1]
    lag_count = impulse.shape[1]
    n_sub = lax.axis_size("sub")
    sub = lax.axis_index("sub")
    all_lags = lag_count * n_sub
    tr = tile_rows
    rows4 = seg_rows // tr
    wide = tr * width
    shift = lag_count // tr
    halo = all_lags // tr
    lag_tiles = shift + 1

    columns = jnp.arange(width, dtype=jnp.int32)
    onehot = (terminal[:, :, None] == columns[None, None, :]).astype(jnp.bfloat16)
    cot4 = cotangent.reshape(rows4, tr, nb, width)
    reord4 = jnp.einsum(
        "ksbi,bir->bksr", cot4, onehot, preferred_element_type=jnp.float32
    ).astype(jnp.bfloat16)
    r4 = reord4.reshape(nb, rows4, wide)
    r4t = jnp.transpose(reord4, (0, 2, 3, 1)).reshape(nb, wide, rows4)

    seg_start = lax.axis_index("tm") * seg_rows
    steps4 = seg_start + tr * jnp.arange(rows4, dtype=jnp.int32)[:, None] + jnp.arange(tr, dtype=jnp.int32)[None, :]
    live4 = steps4 >= fault_step[0]
    inp4 = jnp.transpose(inputs.reshape(rows4, tr, nb, width), (2, 0, 1, 3))
    m4 = jnp.where(live4[None, :, :, None], inp4, jnp.zeros((), jnp.bfloat16)).reshape(nb, rows4, wide)

    ahead = passed_along(r4[:, :halo], "tm", -1)
    r4ext = jnp.concatenate([r4, ahead], axis=1).astype(jnp.float32)
    r4w = lax.dynamic_slice_in_dim(r4ext, sub * shift, rows4 + shift, 1)
    behind = passed_along(m4[:, rows4 - halo :], "tm", 1)
    m4ext = jnp.concatenate([behind, m4], axis=1).astype(jnp.float32)
    m4w = lax.dynamic_slice_in_dim(m4ext, (n_sub - 1 - sub) * shift, rows4 + shift, 1)

    kern = impulse.reshape(nb, lag_count, width, width)
    kpad = jnp.pad(kern, ((0, 0), (tr - 1, tr), (0, 0), (0, 0)))
    stripes = tr * lag_tiles
    toeplitz = jnp.concatenate(
        [lax.slice_in_dim(kpad, tr - 1 - u, tr - 1 - u + stripes, 1, 1) for u in range(tr)], axis=3
    ).reshape(nb, stripes * width, wide)

    partial_dx = pl.pallas_call(
        functools.partial(dx_kernel, lag_tiles=lag_tiles, rows=rows4),
        grid=(nb,),
        in_specs=[
            pl.BlockSpec((1, rows4 + shift, wide), lambda b: (b, 0, 0)),
            pl.BlockSpec((1, tr * lag_tiles * width, wide), lambda b: (b, 0, 0)),
        ],
        out_specs=pl.BlockSpec((1, rows4, wide), lambda b: (b, 0, 0)),
        out_shape=jax.ShapeDtypeStruct((nb, rows4, wide), jnp.float32),
        interpret=_INTERPRET,
    )(r4w, toeplitz)

    raw = pl.pallas_call(
        functools.partial(raw_kernel, shift=shift, rows=rows4, width=width),
        grid=(nb,),
        in_specs=[
            pl.BlockSpec((1, wide, rows4), lambda b: (b, 0, 0)),
            pl.BlockSpec((1, rows4 + shift, wide), lambda b: (b, 0, 0)),
        ],
        out_specs=pl.BlockSpec((1, lag_count, width, width), lambda b: (b, 0, 0, 0)),
        out_shape=jax.ShapeDtypeStruct((nb, lag_count, width, width), jnp.float32),
        interpret=_INTERPRET,
    )(r4t, m4w)

    summed_dx = lax.psum_scatter(partial_dx, "sub", scatter_dimension=1, tiled=True)
    share4 = summed_dx.shape[1]
    own_steps = (
        seg_start
        + sub * share4 * tr
        + tr * jnp.arange(share4, dtype=jnp.int32)[:, None]
        + jnp.arange(tr, dtype=jnp.int32)[None, :]
    )
    dx = jnp.where(
        (own_steps >= fault_step[0])[None, :, :, None],
        summed_dx.reshape(nb, share4, tr, width),
        0.0,
    ).astype(jnp.bfloat16)
    voltage_grad = jnp.transpose(dx, (1, 2, 0, 3)).reshape(share4 * tr, nb * width)

    grad_flat = raw.reshape(nb, lag_count, width * width)
    own_grad = lax.psum_scatter(grad_flat, "tm", scatter_dimension=2, tiled=True)
    own_squares = jnp.sum(own_grad * own_grad)
    total_squares = lax.psum(own_squares, ("tm", "bundle", "sub"))
    norm_limit = norm_ratio * math.sqrt(NB * L * CB * CB)
    factor = norm_limit / jnp.sqrt(total_squares + 1e-06)
    return (voltage_grad, own_grad * factor)


def solution(mesh):
    placed = (
        P(("case", "tm"), "bundle"),
        P(("case", "tm"), "bundle"),
        P("bundle", "sub", None),
        P("bundle", None),
        P("case"),
    )
    return jax.shard_map(
        local,
        mesh=mesh,
        in_specs=placed,
        out_specs=(P(("case", "tm", "sub"), "bundle"), P(("case", "bundle"), "sub", "tm")),
        check_vma=False,
    )
```

```python
import functools
import math

import jax
import jax.numpy as jnp
from jax import lax
from jax.experimental import pallas as pl
from jax.sharding import PartitionSpec as P

CB = 64
NB = 8
L = 128


norm_ratio = 0.5
tile_rows = 4
chunk_rows = 256
_INTERPRET = False


def passed_along(block, axis, distance):
    devices = range(lax.axis_size(axis))
    route = [(i - distance, i) for i in devices if i - distance in devices]
    return lax.ppermute(block, axis, route)


def dx_kernel(r_ref, t_ref, o_ref, *, lag_tiles, rows):
    width = o_ref.shape[2]
    width_t = t_ref.shape[2]
    for c in range(rows // chunk_rows):
        base = c * chunk_rows
        acc = jnp.zeros((chunk_rows, width), jnp.float32)
        for q in range(lag_tiles):
            x = r_ref[0, base + q : base + q + chunk_rows, :].astype(jnp.bfloat16)
            acc = acc + jnp.dot(x, t_ref[0, q * width_t : (q + 1) * width_t, :], preferred_element_type=jnp.float32)
        o_ref[0, base : base + chunk_rows, :] = acc


def raw_kernel(rt_ref, m_ref, o_ref, *, shift, rows, width):
    rt = rt_ref[0]

    def corr(q):
        m = m_ref[0, shift - q : shift - q + rows, :].astype(jnp.bfloat16)
        return jnp.dot(rt, m, preferred_element_type=jnp.float32)

    g_prev = corr(0)
    for a in range(shift):
        g_next = corr(a + 1)
        for d in range(tile_rows):
            acc = None
            for s in range(tile_rows):
                u = s - d
                if 0 <= u < tile_rows:
                    blk = g_prev[s * width : (s + 1) * width, u * width : (u + 1) * width]
                    acc = blk if acc is None else acc + blk
                u = s - d + tile_rows
                if 0 <= u < tile_rows:
                    blk = g_next[s * width : (s + 1) * width, u * width : (u + 1) * width]
                    acc = blk if acc is None else acc + blk
            o_ref[0, tile_rows * a + d] = acc
        g_prev = g_next


def local(cotangent, inputs, impulse, terminal, fault_step):
    seg_rows = cotangent.shape[0]
    nb = terminal.shape[0]
    width = terminal.shape[1]
    lag_count = impulse.shape[1]
    n_sub = lax.axis_size("sub")
    sub = lax.axis_index("sub")
    all_lags = lag_count * n_sub
    tr = tile_rows
    rows4 = seg_rows // tr
    wide = tr * width
    shift = lag_count // tr
    halo = all_lags // tr
    lag_tiles = shift + 1

    columns = jnp.arange(width, dtype=jnp.int32)
    onehot = (terminal[:, :, None] == columns[None, None, :]).astype(jnp.bfloat16)
    cot4 = cotangent.reshape(rows4, tr, nb, width)
    reord4 = jnp.einsum(
        "ksbi,bir->bksr", cot4, onehot, preferred_element_type=jnp.float32
    ).astype(jnp.bfloat16)
    r4 = reord4.reshape(nb, rows4, wide)
    r4t = jnp.transpose(reord4, (0, 2, 3, 1)).reshape(nb, wide, rows4)

    seg_start = lax.axis_index("tm") * seg_rows
    steps4 = seg_start + tr * jnp.arange(rows4, dtype=jnp.int32)[:, None] + jnp.arange(tr, dtype=jnp.int32)[None, :]
    live4 = steps4 >= fault_step[0]
    inp4 = jnp.transpose(inputs.reshape(rows4, tr, nb, width), (2, 0, 1, 3))
    m4 = jnp.where(live4[None, :, :, None], inp4, jnp.zeros((), jnp.bfloat16)).reshape(nb, rows4, wide)

    ahead = passed_along(r4[:, :halo], "tm", -1)
    r4ext = jnp.concatenate([r4, ahead], axis=1).astype(jnp.float32)
    r4w = lax.dynamic_slice_in_dim(r4ext, sub * shift, rows4 + shift, 1)
    behind = passed_along(m4[:, rows4 - halo :], "tm", 1)
    m4ext = jnp.concatenate([behind, m4], axis=1).astype(jnp.float32)
    m4w = lax.dynamic_slice_in_dim(m4ext, (n_sub - 1 - sub) * shift, rows4 + shift, 1)

    kern = impulse.reshape(nb, lag_count, width, width)
    kpad = jnp.pad(kern, ((0, 0), (tr - 1, tr), (0, 0), (0, 0)))
    stripes = tr * lag_tiles
    toeplitz = jnp.concatenate(
        [lax.slice_in_dim(kpad, tr - 1 - u, tr - 1 - u + stripes, 1, 1) for u in range(tr)], axis=3
    ).reshape(nb, stripes * width, wide)

    partial_dx = pl.pallas_call(
        functools.partial(dx_kernel, lag_tiles=lag_tiles, rows=rows4),
        grid=(nb,),
        in_specs=[
            pl.BlockSpec((1, rows4 + shift, wide), lambda b: (b, 0, 0)),
            pl.BlockSpec((1, tr * lag_tiles * width, wide), lambda b: (b, 0, 0)),
        ],
        out_specs=pl.BlockSpec((1, rows4, wide), lambda b: (b, 0, 0)),
        out_shape=jax.ShapeDtypeStruct((nb, rows4, wide), jnp.float32),
        interpret=_INTERPRET,
    )(r4w, toeplitz)

    raw = pl.pallas_call(
        functools.partial(raw_kernel, shift=shift, rows=rows4, width=width),
        grid=(nb,),
        in_specs=[
            pl.BlockSpec((1, wide, rows4), lambda b: (b, 0, 0)),
            pl.BlockSpec((1, rows4 + shift, wide), lambda b: (b, 0, 0)),
        ],
        out_specs=pl.BlockSpec((1, lag_count, width, width), lambda b: (b, 0, 0, 0)),
        out_shape=jax.ShapeDtypeStruct((nb, lag_count, width, width), jnp.float32),
        interpret=_INTERPRET,
    )(r4t, m4w)

    summed_dx = lax.psum_scatter(partial_dx, "sub", scatter_dimension=1, tiled=True)
    share4 = summed_dx.shape[1]
    own_steps = (
        seg_start
        + sub * share4 * tr
        + tr * jnp.arange(share4, dtype=jnp.int32)[:, None]
        + jnp.arange(tr, dtype=jnp.int32)[None, :]
    )
    dx = jnp.where(
        (own_steps >= fault_step[0])[None, :, :, None],
        summed_dx.reshape(nb, share4, tr, width),
        0.0,
    ).astype(jnp.bfloat16)
    voltage_grad = jnp.transpose(dx, (1, 2, 0, 3)).reshape(share4 * tr, nb * width)

    grad_flat = raw.reshape(nb, lag_count, width * width)
    own_grad = lax.psum_scatter(grad_flat, "tm", scatter_dimension=2, tiled=True)
    own_squares = jnp.sum(own_grad * own_grad)
    total_squares = own_squares
    for axis in ("sub", "bundle", "tm"):
        total_squares = lax.psum(total_squares, axis)
    norm_limit = norm_ratio * math.sqrt(NB * L * CB * CB)
    factor = norm_limit / jnp.sqrt(total_squares + 1e-06)
    return (voltage_grad, own_grad * factor)


def solution(mesh):
    placed = (
        P(("case", "tm"), "bundle"),
        P(("case", "tm"), "bundle"),
        P("bundle", "sub", None),
        P("bundle", None),
        P("case"),
    )
    return jax.shard_map(
        local,
        mesh=mesh,
        in_specs=placed,
        out_specs=(P(("case", "tm", "sub"), "bundle"), P(("case", "bundle"), "sub", "tm")),
        check_vma=False,
    )
```

```python
import functools
import math

import jax
import jax.numpy as jnp
from jax import lax
from jax.experimental import pallas as pl
from jax.experimental.pallas import tpu as pltpu
from jax.sharding import PartitionSpec as P

CB = 64
NB = 8
L = 128


norm_ratio = 0.5
tile_rows = 4
chunk_rows = 256
_INTERPRET = False


def passed_along(block, axis, distance):
    devices = range(lax.axis_size(axis))
    route = [(i - distance, i) for i in devices if i - distance in devices]
    return lax.ppermute(block, axis, route)


def lags_span(all_lags, band):
    return band * (all_lags // band + 1) + 1


def dx_kernel(r_ref, t_ref, o_ref, *, lag_tiles, rows):
    width = o_ref.shape[2]
    width_t = t_ref.shape[2]
    for c in range(rows // chunk_rows):
        base = c * chunk_rows
        acc = jnp.zeros((chunk_rows, width), jnp.float32)
        for q in range(lag_tiles):
            x = r_ref[0, base + q : base + q + chunk_rows, :].astype(jnp.bfloat16)
            acc = acc + jnp.dot(x, t_ref[0, q * width_t : (q + 1) * width_t, :], preferred_element_type=jnp.float32)
        o_ref[0, base : base + chunk_rows, :] = acc


def raw_kernel(rt_ref, m_ref, o_ref, acc_ref, *, lag_steps, rows, chunk, pad, lags):
    band = 16
    acc_ref[...] = jnp.zeros(acc_ref.shape, jnp.float32)
    rt = rt_ref[0]
    top = lag_steps - 1
    for q in range(lag_steps):
        m = m_ref[0, top - q : top - q + rows, :].astype(jnp.bfloat16)
        g = jnp.dot(rt, m, preferred_element_type=jnp.float32)
        for v in range(band // 2):
            first = (band * q - 2 * v + pad) * chunk
            acc_ref[first : first + band * chunk, :] += g[:, v * 2 * CB : (v + 1) * 2 * CB]
    lo = acc_ref[pad * chunk : (pad + lags) * chunk, :]
    hi = acc_ref[(pad + 1) * chunk : (pad + 1 + lags) * chunk, :]
    o_ref[0] = lo[:, :CB] + hi[:, CB:]


def local(cotangent, inputs, impulse, terminal, fault_step):
    seg_rows = cotangent.shape[0]
    nb = terminal.shape[0]
    width = terminal.shape[1]
    lag_count = impulse.shape[1]
    n_sub = lax.axis_size("sub")
    sub = lax.axis_index("sub")
    all_lags = lag_count * n_sub
    tr = tile_rows
    rows4 = seg_rows // tr
    wide = tr * width
    shift = lag_count // tr
    halo = all_lags // tr
    lag_tiles = shift + 1

    columns = jnp.arange(width, dtype=jnp.int32)
    onehot = (terminal[:, :, None] == columns[None, None, :]).astype(jnp.bfloat16)
    cot4 = cotangent.reshape(rows4, tr, nb, width)
    reord4 = jnp.einsum(
        "ksbi,bir->bksr", cot4, onehot, preferred_element_type=jnp.float32
    ).astype(jnp.bfloat16)
    r4 = reord4.reshape(nb, rows4, wide)

    seg_start = lax.axis_index("tm") * seg_rows
    steps4 = seg_start + tr * jnp.arange(rows4, dtype=jnp.int32)[:, None] + jnp.arange(tr, dtype=jnp.int32)[None, :]
    live4 = steps4 >= fault_step[0]
    inp4 = jnp.transpose(inputs.reshape(rows4, tr, nb, width), (2, 0, 1, 3))
    m4 = jnp.where(live4[None, :, :, None], inp4, jnp.zeros((), jnp.bfloat16)).reshape(nb, rows4, wide)

    ahead = passed_along(r4[:, :halo], "tm", -1)
    r4ext = jnp.concatenate([r4, ahead], axis=1).astype(jnp.float32)
    r4w = lax.dynamic_slice_in_dim(r4ext, sub * shift, rows4 + shift, 1)
    kern = impulse.reshape(nb, lag_count, width, width)
    kpad = jnp.pad(kern, ((0, 0), (tr - 1, tr), (0, 0), (0, 0)))
    stripes = tr * lag_tiles
    toeplitz = jnp.concatenate(
        [lax.slice_in_dim(kpad, tr - 1 - u, tr - 1 - u + stripes, 1, 1) for u in range(tr)], axis=3
    ).reshape(nb, stripes * width, wide)

    partial_dx = pl.pallas_call(
        functools.partial(dx_kernel, lag_tiles=lag_tiles, rows=rows4),
        grid=(nb,),
        in_specs=[
            pl.BlockSpec((1, rows4 + shift, wide), lambda b: (b, 0, 0)),
            pl.BlockSpec((1, tr * lag_tiles * width, wide), lambda b: (b, 0, 0)),
        ],
        out_specs=pl.BlockSpec((1, rows4, wide), lambda b: (b, 0, 0)),
        out_shape=jax.ShapeDtypeStruct((nb, rows4, wide), jnp.float32),
        interpret=_INTERPRET,
    )(r4w, toeplitz)

    n_tm = lax.axis_size("tm")
    half = nb // n_sub
    chunk = width // n_tm
    band = 16
    rows16 = seg_rows * n_tm // band
    lag_steps = all_lags // band + 1
    pad = band
    mine = lax.dynamic_slice_in_dim(m4.reshape(nb, seg_rows, width), sub * half, half, 0)
    m_all = lax.all_gather(mine, "tm", axis=1, tiled=True)
    m16 = m_all.reshape(half, rows16, band * width)
    m16 = jnp.pad(m16, ((0, 0), (lag_steps - 1, 0), (0, 0))).astype(jnp.float32)
    reord_mine = lax.dynamic_slice_in_dim(r4.reshape(nb, seg_rows, width), sub * half, half, 0)
    r_split = reord_mine.reshape(half, seg_rows, n_tm, chunk)
    r_all = lax.all_to_all(r_split, "tm", 2, 1, tiled=True)
    r16t = jnp.transpose(r_all.reshape(half, rows16, band, chunk), (0, 2, 3, 1)).reshape(half, band * chunk, rows16)
    acc_rows = (pad + lags_span(all_lags, band) + pad) * chunk
    raw_half = pl.pallas_call(
        functools.partial(raw_kernel, lag_steps=lag_steps, rows=rows16, chunk=chunk, pad=pad, lags=all_lags),
        grid=(half,),
        in_specs=[
            pl.BlockSpec((1, band * chunk, rows16), lambda b: (b, 0, 0)),
            pl.BlockSpec((1, rows16 + lag_steps - 1, band * width), lambda b: (b, 0, 0)),
        ],
        out_specs=pl.BlockSpec((1, all_lags * chunk, width), lambda b: (b, 0, 0)),
        out_shape=jax.ShapeDtypeStruct((half, all_lags * chunk, width), jnp.float32),
        scratch_shapes=[pltpu.VMEM((acc_rows, 2 * width), jnp.float32)],
        interpret=_INTERPRET,
    )(r16t, m16)
    raw_half = raw_half.reshape(half, all_lags, chunk * width)
    own_raw = lax.all_to_all(raw_half, "sub", 1, 0, tiled=True)

    summed_dx = lax.psum_scatter(partial_dx, "sub", scatter_dimension=1, tiled=True)
    share4 = summed_dx.shape[1]
    own_steps = (
        seg_start
        + sub * share4 * tr
        + tr * jnp.arange(share4, dtype=jnp.int32)[:, None]
        + jnp.arange(tr, dtype=jnp.int32)[None, :]
    )
    dx = jnp.where(
        (own_steps >= fault_step[0])[None, :, :, None],
        summed_dx.reshape(nb, share4, tr, width),
        0.0,
    ).astype(jnp.bfloat16)
    voltage_grad = jnp.transpose(dx, (1, 2, 0, 3)).reshape(share4 * tr, nb * width)

    own_grad = own_raw
    own_squares = jnp.sum(own_grad * own_grad)
    total_squares = own_squares
    for axis in ("sub", "bundle", "tm"):
        total_squares = lax.psum(total_squares, axis)
    norm_limit = norm_ratio * math.sqrt(NB * L * CB * CB)
    factor = norm_limit / jnp.sqrt(total_squares + 1e-06)
    return (voltage_grad, own_grad * factor)


def solution(mesh):
    placed = (
        P(("case", "tm"), "bundle"),
        P(("case", "tm"), "bundle"),
        P("bundle", "sub", None),
        P("bundle", None),
        P("case"),
    )
    return jax.shard_map(
        local,
        mesh=mesh,
        in_specs=placed,
        out_specs=(P(("case", "tm", "sub"), "bundle"), P(("case", "bundle"), "sub", "tm")),
        check_vma=False,
    )
```

```python
import functools
import math

import jax
import jax.numpy as jnp
from jax import lax
from jax.experimental import pallas as pl
from jax.experimental.pallas import tpu as pltpu
from jax.sharding import PartitionSpec as P

CB = 64
NB = 8
L = 128


norm_ratio = 0.5
tile_rows = 4
chunk_rows = 256
_INTERPRET = False


def passed_along(block, axis, distance):
    devices = range(lax.axis_size(axis))
    route = [(i - distance, i) for i in devices if i - distance in devices]
    return lax.ppermute(block, axis, route)


def lags_span(all_lags, band):
    return band * (all_lags // band + 1) + 1


def dx_kernel(r_ref, t_ref, o_ref, *, lag_tiles, rows):
    width = o_ref.shape[2]
    width_t = t_ref.shape[2]
    for c in range(rows // chunk_rows):
        base = c * chunk_rows
        acc = jnp.zeros((chunk_rows, width), jnp.float32)
        for q in range(lag_tiles):
            x = r_ref[0, base + q : base + q + chunk_rows, :].astype(jnp.bfloat16)
            acc = acc + jnp.dot(x, t_ref[0, q * width_t : (q + 1) * width_t, :], preferred_element_type=jnp.float32)
        o_ref[0, base : base + chunk_rows, :] = acc


def raw_kernel(rt_ref, m_ref, o_ref, acc_ref, *, lag_steps, rows, chunk, pad, lags):
    band = 16
    acc_ref[...] = jnp.zeros(acc_ref.shape, jnp.float32)
    rt = rt_ref[0]
    top = lag_steps - 1
    for q in range(lag_steps):
        m = m_ref[0, top - q : top - q + rows, :].astype(jnp.bfloat16)
        g = jnp.dot(rt, m, preferred_element_type=jnp.float32)
        for v in range(band // 2):
            first = (band * q - 2 * v + pad) * chunk
            acc_ref[first : first + band * chunk, :] += g[:, v * 2 * CB : (v + 1) * 2 * CB]
    lo = acc_ref[pad * chunk : (pad + lags) * chunk, :]
    hi = acc_ref[(pad + 1) * chunk : (pad + 1 + lags) * chunk, :]
    o_ref[0] = lo[:, :CB] + hi[:, CB:]


def local(cotangent, inputs, impulse, terminal, fault_step):
    seg_rows = cotangent.shape[0]
    nb = terminal.shape[0]
    width = terminal.shape[1]
    lag_count = impulse.shape[1]
    n_sub = lax.axis_size("sub")
    sub = lax.axis_index("sub")
    all_lags = lag_count * n_sub
    tr = tile_rows
    rows4 = seg_rows // tr
    wide = tr * width
    shift = lag_count // tr
    halo = all_lags // tr
    lag_tiles = shift + 1

    columns = jnp.arange(width, dtype=jnp.int32)
    onehot = (terminal[:, :, None] == columns[None, None, :]).astype(jnp.bfloat16)
    cot4 = cotangent.reshape(rows4, tr, nb, width)
    reord4 = jnp.einsum(
        "ksbi,bir->bksr", cot4, onehot, preferred_element_type=jnp.float32
    ).astype(jnp.bfloat16)
    r4 = reord4.reshape(nb, rows4, wide)

    seg_start = lax.axis_index("tm") * seg_rows
    steps4 = seg_start + tr * jnp.arange(rows4, dtype=jnp.int32)[:, None] + jnp.arange(tr, dtype=jnp.int32)[None, :]
    live4 = steps4 >= fault_step[0]
    inp4 = jnp.transpose(inputs.reshape(rows4, tr, nb, width), (2, 0, 1, 3))
    m4 = jnp.where(live4[None, :, :, None], inp4, jnp.zeros((), jnp.bfloat16)).reshape(nb, rows4, wide)

    ahead = passed_along(r4[:, :halo], "tm", -1)
    r4ext = jnp.concatenate([r4, ahead], axis=1).astype(jnp.float32)
    r4w = lax.dynamic_slice_in_dim(r4ext, sub * shift, rows4 + shift, 1)
    kern = impulse.reshape(nb, lag_count, width, width)
    kpad = jnp.pad(kern, ((0, 0), (tr - 1, tr), (0, 0), (0, 0)))
    stripes = tr * lag_tiles
    toeplitz = jnp.concatenate(
        [lax.slice_in_dim(kpad, tr - 1 - u, tr - 1 - u + stripes, 1, 1) for u in range(tr)], axis=3
    ).reshape(nb, stripes * width, wide)

    partial_dx = pl.pallas_call(
        functools.partial(dx_kernel, lag_tiles=lag_tiles, rows=rows4),
        grid=(nb,),
        in_specs=[
            pl.BlockSpec((1, rows4 + shift, wide), lambda b: (b, 0, 0)),
            pl.BlockSpec((1, tr * lag_tiles * width, wide), lambda b: (b, 0, 0)),
        ],
        out_specs=pl.BlockSpec((1, rows4, wide), lambda b: (b, 0, 0)),
        out_shape=jax.ShapeDtypeStruct((nb, rows4, wide), jnp.float32),
        interpret=_INTERPRET,
    )(r4w, toeplitz)

    n_tm = lax.axis_size("tm")
    half = nb // n_sub
    chunk = width // n_tm
    band = 16
    rows16 = seg_rows * n_tm // band
    lag_steps = all_lags // band + 1
    pad = band
    mine = lax.dynamic_slice_in_dim(m4.reshape(nb, seg_rows, width), sub * half, half, 0)
    m_all = lax.all_gather(mine, "tm", axis=1, tiled=True)
    m16 = m_all.reshape(half, rows16, band * width)
    m16 = jnp.pad(m16, ((0, 0), (lag_steps - 1, 0), (0, 0))).astype(jnp.float32)
    reord_mine = lax.dynamic_slice_in_dim(r4.reshape(nb, seg_rows, width), sub * half, half, 0)
    r_split = reord_mine.reshape(half, seg_rows, n_tm, chunk)
    tm_idx = lax.axis_index("tm")
    own_piece = lax.dynamic_index_in_dim(r_split, tm_idx, 2, keepdims=False)
    pieces = []
    for e in range(-(n_tm - 1), n_tm):
        if e == 0:
            pieces.append(own_piece)
            continue
        wanted = lax.dynamic_index_in_dim(r_split, jnp.clip(tm_idx - e, 0, n_tm - 1), 2, keepdims=False)
        pieces.append(passed_along(wanted, "tm", -e))
    relative = jnp.concatenate(pieces, axis=1)
    r_all = lax.dynamic_slice_in_dim(relative, (n_tm - 1 - tm_idx) * seg_rows, n_tm * seg_rows, 1)
    r16t = jnp.transpose(r_all.reshape(half, rows16, band, chunk), (0, 2, 3, 1)).reshape(half, band * chunk, rows16)
    acc_rows = (pad + lags_span(all_lags, band) + pad) * chunk
    raw_half = pl.pallas_call(
        functools.partial(raw_kernel, lag_steps=lag_steps, rows=rows16, chunk=chunk, pad=pad, lags=all_lags),
        grid=(half,),
        in_specs=[
            pl.BlockSpec((1, band * chunk, rows16), lambda b: (b, 0, 0)),
            pl.BlockSpec((1, rows16 + lag_steps - 1, band * width), lambda b: (b, 0, 0)),
        ],
        out_specs=pl.BlockSpec((1, all_lags * chunk, width), lambda b: (b, 0, 0)),
        out_shape=jax.ShapeDtypeStruct((half, all_lags * chunk, width), jnp.float32),
        scratch_shapes=[pltpu.VMEM((acc_rows, 2 * width), jnp.float32)],
        interpret=_INTERPRET,
    )(r16t, m16)
    raw_half = raw_half.reshape(half, all_lags, chunk * width)
    own_raw = lax.all_to_all(raw_half, "sub", 1, 0, tiled=True)

    summed_dx = lax.psum_scatter(partial_dx, "sub", scatter_dimension=1, tiled=True)
    share4 = summed_dx.shape[1]
    own_steps = (
        seg_start
        + sub * share4 * tr
        + tr * jnp.arange(share4, dtype=jnp.int32)[:, None]
        + jnp.arange(tr, dtype=jnp.int32)[None, :]
    )
    dx = jnp.where(
        (own_steps >= fault_step[0])[None, :, :, None],
        summed_dx.reshape(nb, share4, tr, width),
        0.0,
    ).astype(jnp.bfloat16)
    voltage_grad = jnp.transpose(dx, (1, 2, 0, 3)).reshape(share4 * tr, nb * width)

    own_grad = own_raw
    own_squares = jnp.sum(own_grad * own_grad)
    total_squares = own_squares
    for axis in ("sub", "bundle", "tm"):
        total_squares = lax.psum(total_squares, axis)
    norm_limit = norm_ratio * math.sqrt(NB * L * CB * CB)
    factor = norm_limit / jnp.sqrt(total_squares + 1e-06)
    return (voltage_grad, own_grad * factor)


def solution(mesh):
    placed = (
        P(("case", "tm"), "bundle"),
        P(("case", "tm"), "bundle"),
        P("bundle", "sub", None),
        P("bundle", None),
        P("case"),
    )
    return jax.shard_map(
        local,
        mesh=mesh,
        in_specs=placed,
        out_specs=(P(("case", "tm", "sub"), "bundle"), P(("case", "bundle"), "sub", "tm")),
        check_vma=False,
    )
```

```python
import functools
import math

import jax
import jax.numpy as jnp
from jax import lax
from jax.experimental import pallas as pl
from jax.experimental.pallas import tpu as pltpu
from jax.sharding import PartitionSpec as P

CB = 64
NB = 8
L = 128


norm_ratio = 0.5
tile_rows = 4
chunk_rows = 256
_INTERPRET = False


def passed_along(block, axis, distance):
    devices = range(lax.axis_size(axis))
    route = [(i - distance, i) for i in devices if i - distance in devices]
    return lax.ppermute(block, axis, route)


def lags_span(all_lags, band):
    return band * (all_lags // band + 1) + 1


def dx_kernel(r_ref, t_ref, o_ref, *, lag_tiles, rows):
    width = o_ref.shape[2]
    width_t = t_ref.shape[2]
    for c in range(rows // chunk_rows):
        base = c * chunk_rows
        acc = jnp.zeros((chunk_rows, width), jnp.float32)
        for q in range(lag_tiles):
            x = r_ref[0, base + q : base + q + chunk_rows, :].astype(jnp.bfloat16)
            acc = acc + jnp.dot(x, t_ref[0, q * width_t : (q + 1) * width_t, :], preferred_element_type=jnp.float32)
        o_ref[0, base : base + chunk_rows, :] = acc


def raw_kernel(rt_ref, m_ref, o_ref, acc_ref, *, lag_steps, rows, chunk, pad, lags):
    band = 16
    acc_ref[...] = jnp.zeros(acc_ref.shape, jnp.float32)
    rt = rt_ref[0]
    top = lag_steps - 1
    for q in range(lag_steps):
        m = m_ref[0, top - q : top - q + rows, :].astype(jnp.bfloat16)
        g = jnp.dot(rt, m, preferred_element_type=jnp.float32)
        for v in range(band // 2):
            first = (band * q - 2 * v + pad) * chunk
            acc_ref[first : first + band * chunk, :] += g[:, v * 2 * CB : (v + 1) * 2 * CB]
    lo = acc_ref[pad * chunk : (pad + lags) * chunk, :]
    hi = acc_ref[(pad + 1) * chunk : (pad + 1 + lags) * chunk, :]
    o_ref[0] = lo[:, :CB] + hi[:, CB:]


def local(cotangent, inputs, impulse, terminal, fault_step):
    seg_rows = cotangent.shape[0]
    nb = terminal.shape[0]
    width = terminal.shape[1]
    lag_count = impulse.shape[1]
    n_sub = lax.axis_size("sub")
    sub = lax.axis_index("sub")
    all_lags = lag_count * n_sub
    tr = tile_rows
    rows4 = seg_rows // tr
    wide = tr * width
    shift = lag_count // tr
    halo = all_lags // tr
    lag_tiles = shift + 1

    columns = jnp.arange(width, dtype=jnp.int32)
    onehot = (terminal[:, :, None] == columns[None, None, :]).astype(jnp.bfloat16)
    cot4 = cotangent.reshape(rows4, tr, nb, width)
    reord4 = jnp.einsum(
        "ksbi,bir->bksr", cot4, onehot, preferred_element_type=jnp.float32
    ).astype(jnp.bfloat16)
    r4 = reord4.reshape(nb, rows4, wide)

    seg_start = lax.axis_index("tm") * seg_rows
    steps4 = seg_start + tr * jnp.arange(rows4, dtype=jnp.int32)[:, None] + jnp.arange(tr, dtype=jnp.int32)[None, :]
    live4 = steps4 >= fault_step[0]
    inp4 = jnp.transpose(inputs.reshape(rows4, tr, nb, width), (2, 0, 1, 3))
    m4 = jnp.where(live4[None, :, :, None], inp4, jnp.zeros((), jnp.bfloat16)).reshape(nb, rows4, wide)

    ahead = passed_along(r4[:, :halo], "tm", -1)
    r4ext = jnp.concatenate([r4, ahead], axis=1).astype(jnp.float32)
    r4w = lax.dynamic_slice_in_dim(r4ext, sub * shift, rows4 + shift, 1)
    kern = impulse.reshape(nb, lag_count, width, width)
    kpad = jnp.pad(kern, ((0, 0), (tr - 1, tr), (0, 0), (0, 0)))
    stripes = tr * lag_tiles
    toeplitz = jnp.concatenate(
        [lax.slice_in_dim(kpad, tr - 1 - u, tr - 1 - u + stripes, 1, 1) for u in range(tr)], axis=3
    ).reshape(nb, stripes * width, wide)

    partial_dx = pl.pallas_call(
        functools.partial(dx_kernel, lag_tiles=lag_tiles, rows=rows4),
        grid=(nb,),
        in_specs=[
            pl.BlockSpec((1, rows4 + shift, wide), lambda b: (b, 0, 0)),
            pl.BlockSpec((1, tr * lag_tiles * width, wide), lambda b: (b, 0, 0)),
        ],
        out_specs=pl.BlockSpec((1, rows4, wide), lambda b: (b, 0, 0)),
        out_shape=jax.ShapeDtypeStruct((nb, rows4, wide), jnp.float32),
        interpret=_INTERPRET,
    )(r4w, toeplitz)

    n_tm = lax.axis_size("tm")
    half = nb // n_sub
    chunk = width // n_tm
    band = 16
    rows16 = seg_rows * n_tm // band
    lag_steps = all_lags // band + 1
    pad = band
    mine = lax.dynamic_slice_in_dim(m4.reshape(nb, seg_rows, width), sub * half, half, 0)
    m_pieces = []
    for e in range(-(n_tm - 1), n_tm):
        m_pieces.append(mine if e == 0 else passed_along(mine, "tm", -e))
    m_relative = jnp.concatenate(m_pieces, axis=1)
    m_all = lax.dynamic_slice_in_dim(m_relative, (n_tm - 1 - lax.axis_index("tm")) * seg_rows, n_tm * seg_rows, 1)
    m16 = m_all.reshape(half, rows16, band * width)
    m16 = jnp.pad(m16, ((0, 0), (lag_steps - 1, 0), (0, 0))).astype(jnp.float32)
    reord_mine = lax.dynamic_slice_in_dim(r4.reshape(nb, seg_rows, width), sub * half, half, 0)
    r_split = reord_mine.reshape(half, seg_rows, n_tm, chunk)
    tm_idx = lax.axis_index("tm")
    own_piece = lax.dynamic_index_in_dim(r_split, tm_idx, 2, keepdims=False)
    pieces = []
    for e in range(-(n_tm - 1), n_tm):
        if e == 0:
            pieces.append(own_piece)
            continue
        wanted = lax.dynamic_index_in_dim(r_split, jnp.clip(tm_idx - e, 0, n_tm - 1), 2, keepdims=False)
        pieces.append(passed_along(wanted, "tm", -e))
    relative = jnp.concatenate(pieces, axis=1)
    r_all = lax.dynamic_slice_in_dim(relative, (n_tm - 1 - tm_idx) * seg_rows, n_tm * seg_rows, 1)
    r16t = jnp.transpose(r_all.reshape(half, rows16, band, chunk), (0, 2, 3, 1)).reshape(half, band * chunk, rows16)
    acc_rows = (pad + lags_span(all_lags, band) + pad) * chunk
    raw_half = pl.pallas_call(
        functools.partial(raw_kernel, lag_steps=lag_steps, rows=rows16, chunk=chunk, pad=pad, lags=all_lags),
        grid=(half,),
        in_specs=[
            pl.BlockSpec((1, band * chunk, rows16), lambda b: (b, 0, 0)),
            pl.BlockSpec((1, rows16 + lag_steps - 1, band * width), lambda b: (b, 0, 0)),
        ],
        out_specs=pl.BlockSpec((1, all_lags * chunk, width), lambda b: (b, 0, 0)),
        out_shape=jax.ShapeDtypeStruct((half, all_lags * chunk, width), jnp.float32),
        scratch_shapes=[pltpu.VMEM((acc_rows, 2 * width), jnp.float32)],
        interpret=_INTERPRET,
    )(r16t, m16)
    raw_half = raw_half.reshape(half, all_lags, chunk * width)
    own_raw = lax.all_to_all(raw_half, "sub", 1, 0, tiled=True)

    summed_dx = lax.psum_scatter(partial_dx, "sub", scatter_dimension=1, tiled=True)
    share4 = summed_dx.shape[1]
    own_steps = (
        seg_start
        + sub * share4 * tr
        + tr * jnp.arange(share4, dtype=jnp.int32)[:, None]
        + jnp.arange(tr, dtype=jnp.int32)[None, :]
    )
    dx = jnp.where(
        (own_steps >= fault_step[0])[None, :, :, None],
        summed_dx.reshape(nb, share4, tr, width),
        0.0,
    ).astype(jnp.bfloat16)
    voltage_grad = jnp.transpose(dx, (1, 2, 0, 3)).reshape(share4 * tr, nb * width)

    own_grad = own_raw
    own_squares = jnp.sum(own_grad * own_grad)
    total_squares = own_squares
    for axis in ("sub", "bundle", "tm"):
        total_squares = lax.psum(total_squares, axis)
    norm_limit = norm_ratio * math.sqrt(NB * L * CB * CB)
    factor = norm_limit / jnp.sqrt(total_squares + 1e-06)
    return (voltage_grad, own_grad * factor)


def solution(mesh):
    placed = (
        P(("case", "tm"), "bundle"),
        P(("case", "tm"), "bundle"),
        P("bundle", "sub", None),
        P("bundle", None),
        P("case"),
    )
    return jax.shard_map(
        local,
        mesh=mesh,
        in_specs=placed,
        out_specs=(P(("case", "tm", "sub"), "bundle"), P(("case", "bundle"), "sub", "tm")),
        check_vma=False,
    )
```

```python
import functools
import math

import jax
import jax.numpy as jnp
from jax import lax
from jax.experimental import pallas as pl
from jax.experimental.pallas import tpu as pltpu
from jax.sharding import PartitionSpec as P

CB = 64
NB = 8
L = 128


norm_ratio = 0.5
tile_rows = 4
chunk_rows = 256
_INTERPRET = False


def passed_along(block, axis, distance):
    devices = range(lax.axis_size(axis))
    route = [(i - distance, i) for i in devices if i - distance in devices]
    return lax.ppermute(block, axis, route)


def lags_span(all_lags, band):
    return band * (all_lags // band + 1) + 1


def dx_kernel(r_ref, t_ref, o_ref, *, lag_tiles, rows):
    width = o_ref.shape[2]
    width_t = t_ref.shape[2]
    for c in range(rows // chunk_rows):
        base = c * chunk_rows
        acc = jnp.zeros((chunk_rows, width), jnp.float32)
        for q in range(lag_tiles):
            x = r_ref[0, base + q : base + q + chunk_rows, :].astype(jnp.bfloat16)
            acc = acc + jnp.dot(x, t_ref[0, q * width_t : (q + 1) * width_t, :], preferred_element_type=jnp.float32)
        o_ref[0, base : base + chunk_rows, :] = acc


def raw_kernel(rt_ref, m_ref, o_ref, acc_ref, *, lag_steps, rows, chunk, pad, lags):
    band = 16
    acc_ref[...] = jnp.zeros(acc_ref.shape, jnp.float32)
    rt = rt_ref[0]
    top = lag_steps - 1
    for q in range(lag_steps):
        m = m_ref[0, top - q : top - q + rows, :].astype(jnp.bfloat16)
        g = jnp.dot(rt, m, preferred_element_type=jnp.float32)
        for v in range(band // 2):
            first = (band * q - 2 * v + pad) * chunk
            acc_ref[first : first + band * chunk, :] += g[:, v * 2 * CB : (v + 1) * 2 * CB]
    lo = acc_ref[pad * chunk : (pad + lags) * chunk, :]
    hi = acc_ref[(pad + 1) * chunk : (pad + 1 + lags) * chunk, :]
    o_ref[0] = lo[:, :CB] + hi[:, CB:]


def local(cotangent, inputs, impulse, terminal, fault_step):
    seg_rows = cotangent.shape[0]
    nb = terminal.shape[0]
    width = terminal.shape[1]
    lag_count = impulse.shape[1]
    n_sub = lax.axis_size("sub")
    sub = lax.axis_index("sub")
    all_lags = lag_count * n_sub
    tr = tile_rows
    rows4 = seg_rows // tr
    wide = tr * width
    shift = lag_count // tr
    halo = all_lags // tr
    lag_tiles = shift + 1

    columns = jnp.arange(width, dtype=jnp.int32)
    onehot = (terminal[:, :, None] == columns[None, None, :]).astype(jnp.bfloat16)
    cot4 = cotangent.reshape(rows4, tr, nb, width)
    reord4 = jnp.einsum(
        "ksbi,bir->bksr", cot4, onehot, preferred_element_type=jnp.float32
    ).astype(jnp.bfloat16)
    r4 = reord4.reshape(nb, rows4, wide)

    seg_start = lax.axis_index("tm") * seg_rows
    steps4 = seg_start + tr * jnp.arange(rows4, dtype=jnp.int32)[:, None] + jnp.arange(tr, dtype=jnp.int32)[None, :]
    live4 = steps4 >= fault_step[0]
    inp4 = jnp.transpose(inputs.reshape(rows4, tr, nb, width), (2, 0, 1, 3))
    m4 = jnp.where(live4[None, :, :, None], inp4, jnp.zeros((), jnp.bfloat16)).reshape(nb, rows4, wide)

    ahead = passed_along(r4[:, :halo], "tm", -1)
    r4ext = jnp.concatenate([r4, ahead], axis=1).astype(jnp.float32)
    r4w = lax.dynamic_slice_in_dim(r4ext, sub * shift, rows4 + shift, 1)
    kern = impulse.reshape(nb, lag_count, width, width)
    kpad = jnp.pad(kern, ((0, 0), (tr - 1, tr), (0, 0), (0, 0)))
    stripes = tr * lag_tiles
    toeplitz = jnp.concatenate(
        [lax.slice_in_dim(kpad, tr - 1 - u, tr - 1 - u + stripes, 1, 1) for u in range(tr)], axis=3
    ).reshape(nb, stripes * width, wide)

    partial_dx = pl.pallas_call(
        functools.partial(dx_kernel, lag_tiles=lag_tiles, rows=rows4),
        grid=(nb,),
        in_specs=[
            pl.BlockSpec((1, rows4 + shift, wide), lambda b: (b, 0, 0)),
            pl.BlockSpec((1, tr * lag_tiles * width, wide), lambda b: (b, 0, 0)),
        ],
        out_specs=pl.BlockSpec((1, rows4, wide), lambda b: (b, 0, 0)),
        out_shape=jax.ShapeDtypeStruct((nb, rows4, wide), jnp.float32),
        interpret=_INTERPRET,
    )(r4w, toeplitz)

    n_tm = lax.axis_size("tm")
    half = nb // n_sub
    chunk = width // n_tm
    band = 16
    rows16 = seg_rows * n_tm // band
    lag_steps = all_lags // band + 1
    pad = band
    seg16 = seg_rows // band
    mine = lax.dynamic_slice_in_dim(m4.reshape(nb, seg_rows, width), sub * half, half, 0)
    m_send = mine.reshape(half, seg16, band * width)
    tm_idx = lax.axis_index("tm")
    m_pieces = []
    for e in range(-(n_tm - 1), n_tm):
        m_pieces.append(m_send if e == 0 else passed_along(m_send, "tm", -e))
    m_relative = jnp.concatenate(m_pieces, axis=1)
    m16 = lax.dynamic_slice_in_dim(m_relative, (n_tm - 1 - tm_idx) * seg16, n_tm * seg16, 1)
    m16 = jnp.pad(m16, ((0, 0), (lag_steps - 1, 0), (0, 0))).astype(jnp.float32)
    reord_mine = lax.dynamic_slice_in_dim(r4.reshape(nb, seg_rows, width), sub * half, half, 0)
    r_split = jnp.transpose(
        reord_mine.reshape(half, seg16, band, n_tm, chunk), (3, 0, 2, 4, 1)
    ).reshape(n_tm, half, band * chunk, seg16)
    own_piece = lax.dynamic_index_in_dim(r_split, tm_idx, 0, keepdims=False)
    pieces = []
    for e in range(-(n_tm - 1), n_tm):
        if e == 0:
            pieces.append(own_piece)
            continue
        wanted = lax.dynamic_index_in_dim(r_split, jnp.clip(tm_idx - e, 0, n_tm - 1), 0, keepdims=False)
        pieces.append(passed_along(wanted, "tm", -e))
    relative = jnp.concatenate(pieces, axis=2)
    r16t = lax.dynamic_slice_in_dim(relative, (n_tm - 1 - tm_idx) * seg16, n_tm * seg16, 2)
    acc_rows = (pad + lags_span(all_lags, band) + pad) * chunk
    raw_half = pl.pallas_call(
        functools.partial(raw_kernel, lag_steps=lag_steps, rows=rows16, chunk=chunk, pad=pad, lags=all_lags),
        grid=(half,),
        in_specs=[
            pl.BlockSpec((1, band * chunk, rows16), lambda b: (b, 0, 0)),
            pl.BlockSpec((1, rows16 + lag_steps - 1, band * width), lambda b: (b, 0, 0)),
        ],
        out_specs=pl.BlockSpec((1, all_lags * chunk, width), lambda b: (b, 0, 0)),
        out_shape=jax.ShapeDtypeStruct((half, all_lags * chunk, width), jnp.float32),
        scratch_shapes=[pltpu.VMEM((acc_rows, 2 * width), jnp.float32)],
        interpret=_INTERPRET,
    )(r16t, m16)
    raw_half = raw_half.reshape(half, all_lags, chunk * width)
    own_raw = lax.all_to_all(raw_half, "sub", 1, 0, tiled=True)

    summed_dx = lax.psum_scatter(partial_dx, "sub", scatter_dimension=1, tiled=True)
    share4 = summed_dx.shape[1]
    own_steps = (
        seg_start
        + sub * share4 * tr
        + tr * jnp.arange(share4, dtype=jnp.int32)[:, None]
        + jnp.arange(tr, dtype=jnp.int32)[None, :]
    )
    dx = jnp.where(
        (own_steps >= fault_step[0])[None, :, :, None],
        summed_dx.reshape(nb, share4, tr, width),
        0.0,
    ).astype(jnp.bfloat16)
    voltage_grad = jnp.transpose(dx, (1, 2, 0, 3)).reshape(share4 * tr, nb * width)

    own_grad = own_raw
    own_squares = jnp.sum(own_grad * own_grad)
    total_squares = own_squares
    for axis in ("sub", "bundle", "tm"):
        total_squares = lax.psum(total_squares, axis)
    norm_limit = norm_ratio * math.sqrt(NB * L * CB * CB)
    factor = norm_limit / jnp.sqrt(total_squares + 1e-06)
    return (voltage_grad, own_grad * factor)


def solution(mesh):
    placed = (
        P(("case", "tm"), "bundle"),
        P(("case", "tm"), "bundle"),
        P("bundle", "sub", None),
        P("bundle", None),
        P("case"),
    )
    return jax.shard_map(
        local,
        mesh=mesh,
        in_specs=placed,
        out_specs=(P(("case", "tm", "sub"), "bundle"), P(("case", "bundle"), "sub", "tm")),
        check_vma=False,
    )
```

```python
import functools
import math

import jax
import jax.numpy as jnp
from jax import lax
from jax.experimental import pallas as pl
from jax.experimental.pallas import tpu as pltpu
from jax.sharding import PartitionSpec as P


CB = 64
NB = 8
L = 128


norm_ratio = 0.5
tile_rows = 4
chunk_rows = 256
_INTERPRET = False


def passed_along(block, axis, distance):
    devices = range(lax.axis_size(axis))
    route = [(i - distance, i) for i in devices if i - distance in devices]
    return lax.ppermute(block, axis, route)


def lags_span(all_lags, band):
    return band * (all_lags // band + 1) + 1


def dx_kernel(r_ref, t_ref, o_ref, *, lag_tiles, rows):
    width = o_ref.shape[2]
    width_t = t_ref.shape[2]
    for c in range(rows // chunk_rows):
        base = c * chunk_rows
        acc = jnp.zeros((chunk_rows, width), jnp.float32)
        for q in range(lag_tiles):
            x = r_ref[0, base + q : base + q + chunk_rows, :].astype(jnp.bfloat16)
            acc = acc + jnp.dot(x, t_ref[0, q * width_t : (q + 1) * width_t, :], preferred_element_type=jnp.float32)
        o_ref[0, base : base + chunk_rows, :] = acc


def raw_kernel(rt_ref, m_ref, o_ref, acc_ref, *, lag_steps, rows, chunk, pad, lags):
    band = 16
    acc_ref[...] = jnp.zeros(acc_ref.shape, jnp.float32)
    rt = jnp.transpose(rt_ref[0]).astype(jnp.bfloat16)
    top = lag_steps - 1
    for q in range(lag_steps):
        m = m_ref[0, top - q : top - q + rows, :].astype(jnp.bfloat16)
        g = jnp.dot(rt, m, preferred_element_type=jnp.float32)
        for v in range(band // 2):
            first = (band * q - 2 * v + pad) * chunk
            acc_ref[first : first + band * chunk, :] += g[:, v * 2 * CB : (v + 1) * 2 * CB]
    lo = acc_ref[pad * chunk : (pad + lags) * chunk, :]
    hi = acc_ref[(pad + 1) * chunk : (pad + 1 + lags) * chunk, :]
    o_ref[0] = lo[:, :CB] + hi[:, CB:]


def local_body(cotangent, inputs, impulse, terminal, fault_step):
    seg_rows = cotangent.shape[0]
    nb = terminal.shape[0]
    width = terminal.shape[1]
    lag_count = impulse.shape[1]
    n_sub = lax.axis_size("sub")
    sub = lax.axis_index("sub")
    all_lags = lag_count * n_sub
    tr = tile_rows
    rows4 = seg_rows // tr
    wide = tr * width
    shift = lag_count // tr
    halo = all_lags // tr
    lag_tiles = shift + 1

    columns = jnp.arange(width, dtype=jnp.int32)
    onehot = (terminal[:, :, None] == columns[None, None, :]).astype(jnp.bfloat16)
    cot4 = cotangent.reshape(rows4, tr, nb, width)
    reord4 = jnp.einsum(
        "ksbi,bir->bksr", cot4, onehot, preferred_element_type=jnp.float32
    ).astype(jnp.bfloat16)
    r4 = reord4.reshape(nb, rows4, wide)

    seg_start = lax.axis_index("tm") * seg_rows
    steps4 = seg_start + tr * jnp.arange(rows4, dtype=jnp.int32)[:, None] + jnp.arange(tr, dtype=jnp.int32)[None, :]
    live4 = steps4 >= fault_step[0]
    inp4 = jnp.transpose(inputs.reshape(rows4, tr, nb, width), (2, 0, 1, 3))
    m4 = jnp.where(live4[None, :, :, None], inp4, jnp.zeros((), jnp.bfloat16)).reshape(nb, rows4, wide)

    ahead = passed_along(r4[:, :halo], "tm", -1)
    r4ext = jnp.concatenate([r4, ahead], axis=1).astype(jnp.float32)
    r4w = lax.dynamic_slice_in_dim(r4ext, sub * shift, rows4 + shift, 1)
    kern = impulse.reshape(nb, lag_count, width, width)
    kpad = jnp.pad(kern, ((0, 0), (tr - 1, tr), (0, 0), (0, 0)))
    stripes = tr * lag_tiles
    toeplitz = jnp.concatenate(
        [lax.slice_in_dim(kpad, tr - 1 - u, tr - 1 - u + stripes, 1, 1) for u in range(tr)], axis=3
    ).reshape(nb, stripes * width, wide)

    partial_dx = pl.pallas_call(
        functools.partial(dx_kernel, lag_tiles=lag_tiles, rows=rows4),
        grid=(nb,),
        in_specs=[
            pl.BlockSpec((1, rows4 + shift, wide), lambda b: (b, 0, 0)),
            pl.BlockSpec((1, tr * lag_tiles * width, wide), lambda b: (b, 0, 0)),
        ],
        out_specs=pl.BlockSpec((1, rows4, wide), lambda b: (b, 0, 0)),
        out_shape=jax.ShapeDtypeStruct((nb, rows4, wide), jnp.float32),
        interpret=_INTERPRET,
    )(r4w, toeplitz)

    n_tm = lax.axis_size("tm")
    half = nb // n_sub
    chunk = width // n_tm
    band = 16
    rows16 = seg_rows * n_tm // band
    lag_steps = all_lags // band + 1
    pad = band
    seg16 = seg_rows // band
    tm_idx = lax.axis_index("tm")
    inp16 = jnp.transpose(inputs.reshape(seg16, band, nb, width), (2, 0, 1, 3))
    inp16 = lax.dynamic_slice_in_dim(inp16, sub * half, half, 0)
    steps16 = seg_start + band * jnp.arange(seg16, dtype=jnp.int32)[:, None] + jnp.arange(band, dtype=jnp.int32)[None, :]
    m_send = jnp.where(
        (steps16 >= fault_step[0])[None, :, :, None], inp16, jnp.zeros((), jnp.bfloat16)
    ).reshape(half, seg16, band * width)
    reord_mine = lax.dynamic_slice_in_dim(r4.reshape(nb, seg_rows, width), sub * half, half, 0)
    r_split = jnp.transpose(
        reord_mine.reshape(half, seg16, band, n_tm, chunk), (3, 0, 1, 2, 4)
    ).reshape(n_tm, half, seg16, band * chunk)
    own_piece = jnp.concatenate([m_send, lax.dynamic_index_in_dim(r_split, tm_idx, 0, keepdims=False)], axis=2)
    pieces = []
    for e in range(-(n_tm - 1), n_tm):
        if e == 0:
            pieces.append(own_piece)
            continue
        wanted = lax.dynamic_index_in_dim(r_split, jnp.clip(tm_idx - e, 0, n_tm - 1), 0, keepdims=False)
        pieces.append(passed_along(jnp.concatenate([m_send, wanted], axis=2), "tm", -e))
    relative = jnp.concatenate(pieces, axis=1)
    both = lax.dynamic_slice_in_dim(relative, (n_tm - 1 - tm_idx) * seg16, n_tm * seg16, 1)
    m16 = jnp.pad(both[:, :, : band * width], ((0, 0), (lag_steps - 1, 0), (0, 0))).astype(jnp.float32)
    r16 = both[:, :, band * width :].astype(jnp.float32)
    acc_rows = (pad + lags_span(all_lags, band) + pad) * chunk
    raw_half = pl.pallas_call(
        functools.partial(raw_kernel, lag_steps=lag_steps, rows=rows16, chunk=chunk, pad=pad, lags=all_lags),
        grid=(half,),
        in_specs=[
            pl.BlockSpec((1, rows16, band * chunk), lambda b: (b, 0, 0)),
            pl.BlockSpec((1, rows16 + lag_steps - 1, band * width), lambda b: (b, 0, 0)),
        ],
        out_specs=pl.BlockSpec((1, all_lags * chunk, width), lambda b: (b, 0, 0)),
        out_shape=jax.ShapeDtypeStruct((half, all_lags * chunk, width), jnp.float32),
        scratch_shapes=[pltpu.VMEM((acc_rows, 2 * width), jnp.float32)],
        interpret=_INTERPRET,
    )(r16, m16)
    raw_half = raw_half.reshape(half, all_lags, chunk * width)
    own_raw = lax.all_to_all(raw_half, "sub", 1, 0, tiled=True)

    summed_dx = lax.psum_scatter(partial_dx, "sub", scatter_dimension=1, tiled=True)
    share4 = summed_dx.shape[1]
    own_steps = (
        seg_start
        + sub * share4 * tr
        + tr * jnp.arange(share4, dtype=jnp.int32)[:, None]
        + jnp.arange(tr, dtype=jnp.int32)[None, :]
    )
    dx = jnp.where(
        (own_steps >= fault_step[0])[None, :, :, None],
        summed_dx.reshape(nb, share4, tr, width),
        0.0,
    ).astype(jnp.bfloat16)
    voltage_grad = jnp.transpose(dx, (1, 2, 0, 3)).reshape(share4 * tr, nb * width)

    own_grad = own_raw
    own_squares = jnp.sum(own_grad * own_grad)
    total_squares = own_squares
    for axis in ("sub", "bundle", "tm"):
        total_squares = lax.psum(total_squares, axis)
    norm_limit = norm_ratio * math.sqrt(NB * L * CB * CB)
    factor = norm_limit / jnp.sqrt(total_squares + 1e-06)
    return (voltage_grad, own_grad * factor)


def solution(mesh):
    placed = (
        P(("case", "tm"), "bundle"),
        P(("case", "tm"), "bundle"),
        P("bundle", "sub", None),
        P("bundle", None),
        P("case"),
    )
    return jax.shard_map(
        local_body,
        mesh=mesh,
        in_specs=placed,
        out_specs=(P(("case", "tm", "sub"), "bundle"), P(("case", "bundle"), "sub", "tm")),
        check_vma=False,
    )
```

```python
import functools
import math

import jax
import jax.numpy as jnp
from jax import lax
from jax.experimental import pallas as pl
from jax.experimental.pallas import tpu as pltpu
from jax.sharding import PartitionSpec as P


CB = 64
NB = 8
L = 128


norm_ratio = 0.5
tile_rows = 4
chunk_rows = 256
_INTERPRET = False


def passed_along(block, axis, distance):
    devices = range(lax.axis_size(axis))
    route = [(i - distance, i) for i in devices if i - distance in devices]
    return lax.ppermute(block, axis, route)


def lags_span(all_lags, band):
    return band * (all_lags // band + 1) + 1


def dx_kernel(r_ref, t_ref, o_ref, *, lag_tiles, rows):
    width = o_ref.shape[2]
    width_t = t_ref.shape[2]
    for c in range(rows // chunk_rows):
        base = c * chunk_rows
        acc = jnp.zeros((chunk_rows, width), jnp.float32)
        for q in range(lag_tiles):
            x = r_ref[0, base + q : base + q + chunk_rows, :].astype(jnp.bfloat16)
            acc = acc + jnp.dot(x, t_ref[0, q * width_t : (q + 1) * width_t, :], preferred_element_type=jnp.float32)
        o_ref[0, base : base + chunk_rows, :] = acc


def raw_kernel(rt_ref, m_ref, o_ref, acc_ref, *, lag_steps, rows, chunk, pad, lags):
    band = 16
    acc_ref[...] = jnp.zeros(acc_ref.shape, jnp.float32)
    rt = rt_ref[0]
    top = lag_steps - 1
    for q in range(lag_steps):
        m = m_ref[0, top - q : top - q + rows, :].astype(jnp.bfloat16)
        g = jnp.dot(rt, m, preferred_element_type=jnp.float32)
        for v in range(band // 2):
            first = (band * q - 2 * v + pad) * chunk
            acc_ref[first : first + band * chunk, :] += g[:, v * 2 * CB : (v + 1) * 2 * CB]
    lo = acc_ref[pad * chunk : (pad + lags) * chunk, :]
    hi = acc_ref[(pad + 1) * chunk : (pad + 1 + lags) * chunk, :]
    o_ref[0] = lo[:, :CB] + hi[:, CB:]


def local_body(cotangent, inputs, impulse, terminal, fault_step):
    seg_rows = cotangent.shape[0]
    nb = terminal.shape[0]
    width = terminal.shape[1]
    lag_count = impulse.shape[1]
    n_sub = lax.axis_size("sub")
    sub = lax.axis_index("sub")
    all_lags = lag_count * n_sub
    tr = tile_rows
    rows4 = seg_rows // tr
    wide = tr * width
    shift = lag_count // tr
    halo = all_lags // tr
    lag_tiles = shift + 1

    columns = jnp.arange(width, dtype=jnp.int32)
    onehot = (terminal[:, :, None] == columns[None, None, :]).astype(jnp.bfloat16)
    cot4 = cotangent.reshape(rows4, tr, nb, width)
    reord4 = jnp.einsum(
        "ksbi,bir->bksr", cot4, onehot, preferred_element_type=jnp.float32
    ).astype(jnp.bfloat16)
    r4 = reord4.reshape(nb, rows4, wide)

    seg_start = lax.axis_index("tm") * seg_rows
    steps4 = seg_start + tr * jnp.arange(rows4, dtype=jnp.int32)[:, None] + jnp.arange(tr, dtype=jnp.int32)[None, :]
    live4 = steps4 >= fault_step[0]
    inp4 = jnp.transpose(inputs.reshape(rows4, tr, nb, width), (2, 0, 1, 3))
    m4 = jnp.where(live4[None, :, :, None], inp4, jnp.zeros((), jnp.bfloat16)).reshape(nb, rows4, wide)

    ahead = passed_along(r4[:, :halo], "tm", -1)
    r4ext = jnp.concatenate([r4, ahead], axis=1).astype(jnp.float32)
    r4w = lax.dynamic_slice_in_dim(r4ext, sub * shift, rows4 + shift, 1)
    kern = impulse.reshape(nb, lag_count, width, width)
    kpad = jnp.pad(kern, ((0, 0), (tr - 1, tr), (0, 0), (0, 0)))
    stripes = tr * lag_tiles
    toeplitz = jnp.concatenate(
        [lax.slice_in_dim(kpad, tr - 1 - u, tr - 1 - u + stripes, 1, 1) for u in range(tr)], axis=3
    ).reshape(nb, stripes * width, wide)

    partial_dx = pl.pallas_call(
        functools.partial(dx_kernel, lag_tiles=lag_tiles, rows=rows4),
        grid=(nb,),
        in_specs=[
            pl.BlockSpec((1, rows4 + shift, wide), lambda b: (b, 0, 0)),
            pl.BlockSpec((1, tr * lag_tiles * width, wide), lambda b: (b, 0, 0)),
        ],
        out_specs=pl.BlockSpec((1, rows4, wide), lambda b: (b, 0, 0)),
        out_shape=jax.ShapeDtypeStruct((nb, rows4, wide), jnp.float32),
        interpret=_INTERPRET,
    )(r4w, toeplitz)

    n_tm = lax.axis_size("tm")
    half = nb // n_sub
    chunk = width // n_tm
    band = 16
    rows16 = seg_rows * n_tm // band
    lag_steps = all_lags // band + 1
    pad = band
    seg16 = seg_rows // band
    mine = lax.dynamic_slice_in_dim(m4.reshape(nb, seg_rows, width), sub * half, half, 0)
    m_send = mine.reshape(half, seg16, band * width)
    tm_idx = lax.axis_index("tm")
    m_pieces = []
    for e in range(-(n_tm - 1), n_tm):
        if e == 0:
            m_pieces.append(m_send)
            continue
        m_pieces.append(passed_along(m_send, "tm", -e))
    m_relative = jnp.concatenate(m_pieces, axis=1)
    m16 = lax.dynamic_slice_in_dim(m_relative, (n_tm - 1 - tm_idx) * seg16, n_tm * seg16, 1)
    m16 = jnp.pad(m16, ((0, 0), (lag_steps - 1, 0), (0, 0))).astype(jnp.float32)
    reord_mine = lax.dynamic_slice_in_dim(r4.reshape(nb, seg_rows, width), sub * half, half, 0)
    r_split = jnp.transpose(
        reord_mine.reshape(half, seg16, band, n_tm, chunk), (3, 0, 2, 4, 1)
    ).reshape(n_tm, half, band * chunk, seg16)
    own_piece = lax.dynamic_index_in_dim(r_split, tm_idx, 0, keepdims=False)
    pieces = []
    for e in range(-(n_tm - 1), n_tm):
        if e == 0:
            pieces.append(own_piece)
            continue
        wanted = lax.dynamic_index_in_dim(r_split, jnp.clip(tm_idx - e, 0, n_tm - 1), 0, keepdims=False)
        pieces.append(passed_along(wanted, "tm", -e))
    relative = jnp.concatenate(pieces, axis=2)
    r16t = lax.dynamic_slice_in_dim(relative, (n_tm - 1 - tm_idx) * seg16, n_tm * seg16, 2)
    acc_rows = (pad + lags_span(all_lags, band) + pad) * chunk
    raw_half = pl.pallas_call(
        functools.partial(raw_kernel, lag_steps=lag_steps, rows=rows16, chunk=chunk, pad=pad, lags=all_lags),
        grid=(half,),
        in_specs=[
            pl.BlockSpec((1, band * chunk, rows16), lambda b: (b, 0, 0)),
            pl.BlockSpec((1, rows16 + lag_steps - 1, band * width), lambda b: (b, 0, 0)),
        ],
        out_specs=pl.BlockSpec((1, all_lags * chunk, width), lambda b: (b, 0, 0)),
        out_shape=jax.ShapeDtypeStruct((half, all_lags * chunk, width), jnp.float32),
        scratch_shapes=[pltpu.VMEM((acc_rows, 2 * width), jnp.float32)],
        interpret=_INTERPRET,
    )(r16t, m16)
    raw_half = raw_half.reshape(half, all_lags, chunk * width)
    own_raw = lax.all_to_all(raw_half, "sub", 1, 0, tiled=True)

    summed_dx = lax.psum_scatter(partial_dx, "sub", scatter_dimension=1, tiled=True)
    share4 = summed_dx.shape[1]
    own_steps = (
        seg_start
        + sub * share4 * tr
        + tr * jnp.arange(share4, dtype=jnp.int32)[:, None]
        + jnp.arange(tr, dtype=jnp.int32)[None, :]
    )
    dx = jnp.where(
        (own_steps >= fault_step[0])[None, :, :, None],
        summed_dx.reshape(nb, share4, tr, width),
        0.0,
    ).astype(jnp.bfloat16)
    voltage_grad = jnp.transpose(dx, (1, 2, 0, 3)).reshape(share4 * tr, nb * width)

    own_grad = own_raw
    own_squares = jnp.sum(own_grad * own_grad)
    total_squares = own_squares
    for axis in ("sub", "bundle", "tm"):
        total_squares = lax.psum(total_squares, axis)
    norm_limit = norm_ratio * math.sqrt(NB * L * CB * CB)
    factor = norm_limit / jnp.sqrt(total_squares + 1e-06)
    return (voltage_grad, own_grad * factor)


def solution(mesh):
    placed = (
        P(("case", "tm"), "bundle"),
        P(("case", "tm"), "bundle"),
        P("bundle", "sub", None),
        P("bundle", None),
        P("case"),
    )
    return jax.shard_map(
        local_body,
        mesh=mesh,
        in_specs=placed,
        out_specs=(P(("case", "tm", "sub"), "bundle"), P(("case", "bundle"), "sub", "tm")),
        check_vma=False,
    )
```

```python
import functools
import math

import jax
import jax.numpy as jnp
from jax import lax
from jax.experimental import pallas as pl
from jax.experimental.pallas import tpu as pltpu
from jax.sharding import PartitionSpec as P


CB = 64
NB = 8
L = 128


norm_ratio = 0.5
tile_rows = 4
chunk_rows = 256
_INTERPRET = False


def passed_along(block, axis, distance):
    devices = range(lax.axis_size(axis))
    route = [(i - distance, i) for i in devices if i - distance in devices]
    return lax.ppermute(block, axis, route)


def lags_span(all_lags, band):
    return band * (all_lags // band + 1) + 1


def dx_kernel(r_ref, t_ref, o_ref, *, lag_tiles, rows):
    width = o_ref.shape[2]
    width_t = t_ref.shape[2]
    for c in range(rows // chunk_rows):
        base = c * chunk_rows
        acc = jnp.zeros((chunk_rows, width), jnp.float32)
        for q in range(lag_tiles):
            x = r_ref[0, base + q : base + q + chunk_rows, :].astype(jnp.bfloat16)
            acc = acc + jnp.dot(x, t_ref[0, q * width_t : (q + 1) * width_t, :], preferred_element_type=jnp.float32)
        o_ref[0, base : base + chunk_rows, :] = acc


def raw_kernel(rt_ref, m_ref, o_ref, acc_ref, *, lag_steps, rows, chunk, pad, lags):
    band = 16
    acc_ref[...] = jnp.zeros(acc_ref.shape, jnp.float32)
    rt = rt_ref[0]
    top = lag_steps - 1
    for q in range(lag_steps):
        m = m_ref[0, top - q : top - q + rows, :].astype(jnp.bfloat16)
        g = jnp.dot(rt, m, preferred_element_type=jnp.float32)
        for v in range(band // 2):
            first = (band * q - 2 * v + pad) * chunk
            acc_ref[first : first + band * chunk, :] += g[:, v * 2 * CB : (v + 1) * 2 * CB]
    lo = acc_ref[pad * chunk : (pad + lags) * chunk, :]
    hi = acc_ref[(pad + 1) * chunk : (pad + 1 + lags) * chunk, :]
    o_ref[0] = lo[:, :CB] + hi[:, CB:]


def local_body(cotangent, inputs, impulse, terminal, fault_step):
    seg_rows = cotangent.shape[0]
    nb = terminal.shape[0]
    width = terminal.shape[1]
    lag_count = impulse.shape[1]
    n_sub = lax.axis_size("sub")
    sub = lax.axis_index("sub")
    all_lags = lag_count * n_sub
    tr = tile_rows
    rows4 = seg_rows // tr
    wide = tr * width
    shift = lag_count // tr
    halo = all_lags // tr
    lag_tiles = shift + 1

    columns = jnp.arange(width, dtype=jnp.int32)
    onehot = (terminal[:, :, None] == columns[None, None, :]).astype(jnp.bfloat16)
    cot4 = cotangent.reshape(rows4, tr, nb, width)
    reord4 = jnp.einsum(
        "ksbi,bir->bksr", cot4, onehot, preferred_element_type=jnp.float32
    ).astype(jnp.bfloat16)
    r4 = reord4.reshape(nb, rows4, wide)

    seg_start = lax.axis_index("tm") * seg_rows
    ahead = passed_along(r4[:, :halo], "tm", -1)
    r4ext = jnp.concatenate([r4, ahead], axis=1).astype(jnp.float32)
    r4w = lax.dynamic_slice_in_dim(r4ext, sub * shift, rows4 + shift, 1)
    kern = impulse.reshape(nb, lag_count, width, width)
    kpad = jnp.pad(kern, ((0, 0), (tr - 1, tr), (0, 0), (0, 0)))
    stripes = tr * lag_tiles
    toeplitz = jnp.concatenate(
        [lax.slice_in_dim(kpad, tr - 1 - u, tr - 1 - u + stripes, 1, 1) for u in range(tr)], axis=3
    ).reshape(nb, stripes * width, wide)

    partial_dx = pl.pallas_call(
        functools.partial(dx_kernel, lag_tiles=lag_tiles, rows=rows4),
        grid=(nb,),
        in_specs=[
            pl.BlockSpec((1, rows4 + shift, wide), lambda b: (b, 0, 0)),
            pl.BlockSpec((1, tr * lag_tiles * width, wide), lambda b: (b, 0, 0)),
        ],
        out_specs=pl.BlockSpec((1, rows4, wide), lambda b: (b, 0, 0)),
        out_shape=jax.ShapeDtypeStruct((nb, rows4, wide), jnp.float32),
        interpret=_INTERPRET,
    )(r4w, toeplitz)

    n_tm = lax.axis_size("tm")
    half = nb // n_sub
    chunk = width // n_tm
    band = 16
    rows16 = seg_rows * n_tm // band
    lag_steps = all_lags // band + 1
    pad = band
    seg16 = seg_rows // band
    inp16 = jnp.transpose(inputs.reshape(seg16, band, nb, width), (2, 0, 1, 3))
    inp16 = lax.dynamic_slice_in_dim(inp16, sub * half, half, 0)
    steps16 = seg_start + band * jnp.arange(seg16, dtype=jnp.int32)[:, None] + jnp.arange(band, dtype=jnp.int32)[None, :]
    m_send = jnp.where(
        (steps16 >= fault_step[0])[None, :, :, None], inp16, jnp.zeros((), jnp.bfloat16)
    ).reshape(half, seg16, band * width)
    tm_idx = lax.axis_index("tm")
    m_pieces = []
    for e in range(-(n_tm - 1), n_tm):
        if e == 0:
            m_pieces.append(m_send)
            continue
        m_pieces.append(passed_along(m_send, "tm", -e))
    m_relative = jnp.concatenate(m_pieces, axis=1)
    m16 = lax.dynamic_slice_in_dim(m_relative, (n_tm - 1 - tm_idx) * seg16, n_tm * seg16, 1)
    m16 = jnp.pad(m16, ((0, 0), (lag_steps - 1, 0), (0, 0))).astype(jnp.float32)
    cot16 = lax.dynamic_slice_in_dim(cotangent.reshape(seg16, band, nb, width), sub * half, half, 2)
    onehot_mine = lax.dynamic_slice_in_dim(onehot, sub * half, half, 0).reshape(half, width, n_tm, chunk)
    r_split = jnp.einsum(
        "ksbi,bicr->cbsrk", cot16, onehot_mine, preferred_element_type=jnp.float32
    ).astype(jnp.bfloat16).reshape(n_tm, half, band * chunk, seg16)
    own_piece = lax.dynamic_index_in_dim(r_split, tm_idx, 0, keepdims=False)
    pieces = []
    for e in range(-(n_tm - 1), n_tm):
        if e == 0:
            pieces.append(own_piece)
            continue
        wanted = lax.dynamic_index_in_dim(r_split, jnp.clip(tm_idx - e, 0, n_tm - 1), 0, keepdims=False)
        pieces.append(passed_along(wanted, "tm", -e))
    relative = jnp.concatenate(pieces, axis=2)
    r16t = lax.dynamic_slice_in_dim(relative, (n_tm - 1 - tm_idx) * seg16, n_tm * seg16, 2)
    acc_rows = (pad + lags_span(all_lags, band) + pad) * chunk
    raw_half = pl.pallas_call(
        functools.partial(raw_kernel, lag_steps=lag_steps, rows=rows16, chunk=chunk, pad=pad, lags=all_lags),
        grid=(half,),
        in_specs=[
            pl.BlockSpec((1, band * chunk, rows16), lambda b: (b, 0, 0)),
            pl.BlockSpec((1, rows16 + lag_steps - 1, band * width), lambda b: (b, 0, 0)),
        ],
        out_specs=pl.BlockSpec((1, all_lags * chunk, width), lambda b: (b, 0, 0)),
        out_shape=jax.ShapeDtypeStruct((half, all_lags * chunk, width), jnp.float32),
        scratch_shapes=[pltpu.VMEM((acc_rows, 2 * width), jnp.float32)],
        interpret=_INTERPRET,
    )(r16t, m16)
    raw_half = raw_half.reshape(half, all_lags, chunk * width)
    own_raw = lax.all_to_all(raw_half, "sub", 1, 0, tiled=True)

    summed_dx = lax.psum_scatter(partial_dx, "sub", scatter_dimension=1, tiled=True)
    share4 = summed_dx.shape[1]
    own_steps = (
        seg_start
        + sub * share4 * tr
        + tr * jnp.arange(share4, dtype=jnp.int32)[:, None]
        + jnp.arange(tr, dtype=jnp.int32)[None, :]
    )
    dx = jnp.where(
        (own_steps >= fault_step[0])[None, :, :, None],
        summed_dx.reshape(nb, share4, tr, width),
        0.0,
    ).astype(jnp.bfloat16)
    voltage_grad = jnp.transpose(dx, (1, 2, 0, 3)).reshape(share4 * tr, nb * width)

    own_grad = own_raw
    own_squares = jnp.sum(own_grad * own_grad)
    total_squares = lax.psum(lax.psum(own_squares, ("bundle", "sub")), "tm")
    norm_limit = norm_ratio * math.sqrt(NB * L * CB * CB)
    factor = norm_limit / jnp.sqrt(total_squares + 1e-06)
    return (voltage_grad, own_grad * factor)


def solution(mesh):
    placed = (
        P(("case", "tm"), "bundle"),
        P(("case", "tm"), "bundle"),
        P("bundle", "sub", None),
        P("bundle", None),
        P("case"),
    )
    return jax.shard_map(
        local_body,
        mesh=mesh,
        in_specs=placed,
        out_specs=(P(("case", "tm", "sub"), "bundle"), P(("case", "bundle"), "sub", "tm")),
        check_vma=False,
    )
```

```python
import functools
import math

import jax
import jax.numpy as jnp
from jax import lax
from jax.experimental import pallas as pl
from jax.experimental.pallas import tpu as pltpu
from jax.sharding import PartitionSpec as P


CB = 64
NB = 8
L = 128


norm_ratio = 0.5
tile_rows = 4
chunk_rows = 512
_INTERPRET = False


def passed_along(block, axis, distance):
    devices = range(lax.axis_size(axis))
    route = [(i - distance, i) for i in devices if i - distance in devices]
    return lax.ppermute(block, axis, route)


def lags_span(all_lags, band):
    return band * (all_lags // band + 1) + 1


def dx_kernel(r_ref, t_ref, o_ref, *, lag_tiles, rows):
    width = o_ref.shape[2]
    width_t = t_ref.shape[2]
    for c in range(rows // chunk_rows):
        base = c * chunk_rows
        acc = jnp.zeros((chunk_rows, width), jnp.float32)
        for q in range(lag_tiles):
            x = r_ref[0, base + q : base + q + chunk_rows, :].astype(jnp.bfloat16)
            acc = acc + jnp.dot(x, t_ref[0, q * width_t : (q + 1) * width_t, :], preferred_element_type=jnp.float32)
        o_ref[0, base : base + chunk_rows, :] = acc


def raw_kernel(rt_ref, m_ref, o_ref, acc_ref, *, lag_steps, rows, chunk, pad, lags):
    band = 16
    acc_ref[...] = jnp.zeros(acc_ref.shape, jnp.float32)
    rt = rt_ref[0]
    top = lag_steps - 1
    for q in range(lag_steps):
        m = m_ref[0, top - q : top - q + rows, :].astype(jnp.bfloat16)
        g = jnp.dot(rt, m, preferred_element_type=jnp.float32)
        for v in range(band // 2):
            first = (band * q - 2 * v + pad) * chunk
            acc_ref[first : first + band * chunk, :] += g[:, v * 2 * CB : (v + 1) * 2 * CB]
    lo = acc_ref[pad * chunk : (pad + lags) * chunk, :]
    hi = acc_ref[(pad + 1) * chunk : (pad + 1 + lags) * chunk, :]
    o_ref[0] = lo[:, :CB] + hi[:, CB:]


def local_body(cotangent, inputs, impulse, terminal, fault_step):
    seg_rows = cotangent.shape[0]
    nb = terminal.shape[0]
    width = terminal.shape[1]
    lag_count = impulse.shape[1]
    n_sub = lax.axis_size("sub")
    sub = lax.axis_index("sub")
    all_lags = lag_count * n_sub
    tr = tile_rows
    rows4 = seg_rows // tr
    wide = tr * width
    shift = lag_count // tr
    halo = all_lags // tr
    lag_tiles = shift + 1

    columns = jnp.arange(width, dtype=jnp.int32)
    onehot = (terminal[:, :, None] == columns[None, None, :]).astype(jnp.bfloat16)
    cot4 = cotangent.reshape(rows4, tr, nb, width)
    reord4 = jnp.einsum(
        "ksbi,bir->bksr", cot4, onehot, preferred_element_type=jnp.float32
    ).astype(jnp.bfloat16)
    r4 = reord4.reshape(nb, rows4, wide)

    seg_start = lax.axis_index("tm") * seg_rows
    ahead = passed_along(r4[:, :halo], "tm", -1)
    r4ext = jnp.concatenate([r4, ahead], axis=1).astype(jnp.float32)
    r4w = lax.dynamic_slice_in_dim(r4ext, sub * shift, rows4 + shift, 1)
    kern = impulse.reshape(nb, lag_count, width, width)
    kpad = jnp.pad(kern, ((0, 0), (tr - 1, tr), (0, 0), (0, 0)))
    stripes = tr * lag_tiles
    toeplitz = jnp.concatenate(
        [lax.slice_in_dim(kpad, tr - 1 - u, tr - 1 - u + stripes, 1, 1) for u in range(tr)], axis=3
    ).reshape(nb, stripes * width, wide)

    partial_dx = pl.pallas_call(
        functools.partial(dx_kernel, lag_tiles=lag_tiles, rows=rows4),
        grid=(nb,),
        in_specs=[
            pl.BlockSpec((1, rows4 + shift, wide), lambda b: (b, 0, 0)),
            pl.BlockSpec((1, tr * lag_tiles * width, wide), lambda b: (b, 0, 0)),
        ],
        out_specs=pl.BlockSpec((1, rows4, wide), lambda b: (b, 0, 0)),
        out_shape=jax.ShapeDtypeStruct((nb, rows4, wide), jnp.float32),
        interpret=_INTERPRET,
    )(r4w, toeplitz)

    n_tm = lax.axis_size("tm")
    half = nb // n_sub
    chunk = width // n_tm
    band = 16
    rows16 = seg_rows * n_tm // band
    lag_steps = all_lags // band + 1
    pad = band
    seg16 = seg_rows // band
    inp16 = jnp.transpose(inputs.reshape(seg16, band, nb, width), (2, 0, 1, 3))
    inp16 = lax.dynamic_slice_in_dim(inp16, sub * half, half, 0)
    steps16 = seg_start + band * jnp.arange(seg16, dtype=jnp.int32)[:, None] + jnp.arange(band, dtype=jnp.int32)[None, :]
    m_send = jnp.where(
        (steps16 >= fault_step[0])[None, :, :, None], inp16, jnp.zeros((), jnp.bfloat16)
    ).reshape(half, seg16, band * width)
    tm_idx = lax.axis_index("tm")
    m_pieces = []
    for e in range(-(n_tm - 1), n_tm):
        if e == 0:
            m_pieces.append(m_send)
            continue
        m_pieces.append(passed_along(m_send, "tm", -e))
    m_relative = jnp.concatenate(m_pieces, axis=1)
    m16 = lax.dynamic_slice_in_dim(m_relative, (n_tm - 1 - tm_idx) * seg16, n_tm * seg16, 1)
    m16 = jnp.pad(m16, ((0, 0), (lag_steps - 1, 0), (0, 0))).astype(jnp.float32)
    reord_mine = lax.dynamic_slice_in_dim(r4.reshape(nb, seg_rows, width), sub * half, half, 0)
    r_split = jnp.transpose(
        reord_mine.reshape(half, seg16, band, n_tm, chunk), (3, 0, 2, 4, 1)
    ).reshape(n_tm, half, band * chunk, seg16)
    own_piece = lax.dynamic_index_in_dim(r_split, tm_idx, 0, keepdims=False)
    pieces = []
    for e in range(-(n_tm - 1), n_tm):
        if e == 0:
            pieces.append(own_piece)
            continue
        wanted = lax.dynamic_index_in_dim(r_split, jnp.clip(tm_idx - e, 0, n_tm - 1), 0, keepdims=False)
        pieces.append(passed_along(wanted, "tm", -e))
    relative = jnp.concatenate(pieces, axis=2)
    r16t = lax.dynamic_slice_in_dim(relative, (n_tm - 1 - tm_idx) * seg16, n_tm * seg16, 2)
    acc_rows = (pad + lags_span(all_lags, band) + pad) * chunk
    raw_half = pl.pallas_call(
        functools.partial(raw_kernel, lag_steps=lag_steps, rows=rows16, chunk=chunk, pad=pad, lags=all_lags),
        grid=(half,),
        in_specs=[
            pl.BlockSpec((1, band * chunk, rows16), lambda b: (b, 0, 0)),
            pl.BlockSpec((1, rows16 + lag_steps - 1, band * width), lambda b: (b, 0, 0)),
        ],
        out_specs=pl.BlockSpec((1, all_lags * chunk, width), lambda b: (b, 0, 0)),
        out_shape=jax.ShapeDtypeStruct((half, all_lags * chunk, width), jnp.float32),
        scratch_shapes=[pltpu.VMEM((acc_rows, 2 * width), jnp.float32)],
        interpret=_INTERPRET,
    )(r16t, m16)
    raw_half = raw_half.reshape(half, all_lags, chunk * width)
    own_raw = lax.all_to_all(raw_half, "sub", 1, 0, tiled=True)

    summed_dx = lax.psum_scatter(partial_dx, "sub", scatter_dimension=1, tiled=True)
    share4 = summed_dx.shape[1]
    own_steps = (
        seg_start
        + sub * share4 * tr
        + tr * jnp.arange(share4, dtype=jnp.int32)[:, None]
        + jnp.arange(tr, dtype=jnp.int32)[None, :]
    )
    dx = jnp.where(
        (own_steps >= fault_step[0])[None, :, :, None],
        summed_dx.reshape(nb, share4, tr, width),
        0.0,
    ).astype(jnp.bfloat16)
    voltage_grad = jnp.transpose(dx, (1, 2, 0, 3)).reshape(share4 * tr, nb * width)

    own_grad = own_raw
    own_squares = jnp.sum(own_grad * own_grad)
    total_squares = lax.psum(lax.psum(own_squares, ("bundle", "sub")), "tm")
    norm_limit = norm_ratio * math.sqrt(NB * L * CB * CB)
    factor = norm_limit / jnp.sqrt(total_squares + 1e-06)
    return (voltage_grad, own_grad * factor)


def solution(mesh):
    placed = (
        P(("case", "tm"), "bundle"),
        P(("case", "tm"), "bundle"),
        P("bundle", "sub", None),
        P("bundle", None),
        P("case"),
    )
    return jax.shard_map(
        local_body,
        mesh=mesh,
        in_specs=placed,
        out_specs=(P(("case", "tm", "sub"), "bundle"), P(("case", "bundle"), "sub", "tm")),
        check_vma=False,
    )
```

```python
import functools
import math

import jax
import jax.numpy as jnp
from jax import lax
from jax.experimental import pallas as pl
from jax.experimental.pallas import tpu as pltpu
from jax.sharding import PartitionSpec as P


CB = 64
NB = 8
L = 128


norm_ratio = 0.5
tile_rows = 4
chunk_rows = 512
_INTERPRET = False


def passed_along(block, axis, distance):
    devices = range(lax.axis_size(axis))
    route = [(i - distance, i) for i in devices if i - distance in devices]
    return lax.ppermute(block, axis, route)


def lags_span(all_lags, band):
    return band * (all_lags // band + 1) + 1


def dx_kernel(r_ref, t_ref, o_ref, *, lag_tiles, rows):
    width = o_ref.shape[2]
    cb = t_ref.shape[2]
    for c in range(rows // chunk_rows):
        base = c * chunk_rows
        acc = jnp.zeros((chunk_rows, width), jnp.float32)
        for q in range(lag_tiles):
            x = r_ref[0, base + q : base + q + chunk_rows, :].astype(jnp.bfloat16)
            blk = jnp.concatenate(
                [t_ref[0, (tile_rows * q + tile_rows - 1 - u) * cb : (tile_rows * q + 2 * tile_rows - 1 - u) * cb, :] for u in range(tile_rows)],
                axis=1,
            )
            acc = acc + jnp.dot(x, blk, preferred_element_type=jnp.float32)
        o_ref[0, base : base + chunk_rows, :] = acc


def raw_kernel(rt_ref, m_ref, o_ref, acc_ref, *, lag_steps, rows, chunk, pad, lags):
    band = 16
    acc_ref[...] = jnp.zeros(acc_ref.shape, jnp.float32)
    rt = rt_ref[0]
    top = lag_steps - 1
    for q in range(lag_steps):
        m = m_ref[0, top - q : top - q + rows, :].astype(jnp.bfloat16)
        g = jnp.dot(rt, m, preferred_element_type=jnp.float32)
        for v in range(band // 2):
            first = (band * q - 2 * v + pad) * chunk
            acc_ref[first : first + band * chunk, :] += g[:, v * 2 * CB : (v + 1) * 2 * CB]
    lo = acc_ref[pad * chunk : (pad + lags) * chunk, :]
    hi = acc_ref[(pad + 1) * chunk : (pad + 1 + lags) * chunk, :]
    o_ref[0] = lo[:, :CB] + hi[:, CB:]


def local_body(cotangent, inputs, impulse, terminal, fault_step):
    seg_rows = cotangent.shape[0]
    nb = terminal.shape[0]
    width = terminal.shape[1]
    lag_count = impulse.shape[1]
    n_sub = lax.axis_size("sub")
    sub = lax.axis_index("sub")
    all_lags = lag_count * n_sub
    tr = tile_rows
    rows4 = seg_rows // tr
    wide = tr * width
    shift = lag_count // tr
    halo = all_lags // tr
    lag_tiles = shift + 1

    columns = jnp.arange(width, dtype=jnp.int32)
    onehot = (terminal[:, :, None] == columns[None, None, :]).astype(jnp.bfloat16)
    cot4 = cotangent.reshape(rows4, tr, nb, width)
    reord4 = jnp.einsum(
        "ksbi,bir->bksr", cot4, onehot, preferred_element_type=jnp.float32
    ).astype(jnp.bfloat16)
    r4 = reord4.reshape(nb, rows4, wide)

    seg_start = lax.axis_index("tm") * seg_rows
    ahead = passed_along(r4[:, :halo], "tm", -1)
    r4ext = jnp.concatenate([r4, ahead], axis=1)
    r4w = lax.dynamic_slice_in_dim(r4ext, sub * shift, rows4 + shift, 1)
    kern = impulse.reshape(nb, lag_count, width, width)
    kpad = jnp.pad(kern, ((0, 0), (tr - 1, tr), (0, 0), (0, 0)))
    toeplitz = kpad.reshape(nb, (lag_count + 2 * tr - 1) * width, width)

    partial_dx = pl.pallas_call(
        functools.partial(dx_kernel, lag_tiles=lag_tiles, rows=rows4),
        grid=(nb,),
        in_specs=[
            pl.BlockSpec((1, rows4 + shift, wide), lambda b: (b, 0, 0)),
            pl.BlockSpec((1, (lag_count + 2 * tr - 1) * width, width), lambda b: (b, 0, 0)),
        ],
        out_specs=pl.BlockSpec((1, rows4, wide), lambda b: (b, 0, 0)),
        out_shape=jax.ShapeDtypeStruct((nb, rows4, wide), jnp.float32),
        interpret=_INTERPRET,
    )(r4w, toeplitz)

    n_tm = lax.axis_size("tm")
    half = nb // n_sub
    chunk = width // n_tm
    band = 16
    rows16 = seg_rows * n_tm // band
    lag_steps = all_lags // band + 1
    pad = band
    seg16 = seg_rows // band
    inp16 = jnp.transpose(inputs.reshape(seg16, band, nb, width), (2, 0, 1, 3))
    inp16 = lax.dynamic_slice_in_dim(inp16, sub * half, half, 0)
    steps16 = seg_start + band * jnp.arange(seg16, dtype=jnp.int32)[:, None] + jnp.arange(band, dtype=jnp.int32)[None, :]
    m_send = jnp.where(
        (steps16 >= fault_step[0])[None, :, :, None], inp16, jnp.zeros((), jnp.bfloat16)
    ).reshape(half, seg16, band * width)
    tm_idx = lax.axis_index("tm")
    m_pieces = []
    for e in range(-(n_tm - 1), n_tm):
        if e == 0:
            m_pieces.append(m_send)
            continue
        m_pieces.append(passed_along(m_send, "tm", -e))
    m_relative = jnp.concatenate(m_pieces, axis=1)
    m16 = lax.dynamic_slice_in_dim(m_relative, (n_tm - 1 - tm_idx) * seg16, n_tm * seg16, 1)
    m16 = jnp.pad(m16, ((0, 0), (lag_steps - 1, 0), (0, 0))).astype(jnp.float32)
    reord_mine = lax.dynamic_slice_in_dim(r4.reshape(nb, seg_rows, width), sub * half, half, 0)
    r_split = jnp.transpose(
        reord_mine.reshape(half, seg16, band, n_tm, chunk), (3, 0, 2, 4, 1)
    ).reshape(n_tm, half, band * chunk, seg16)
    own_piece = lax.dynamic_index_in_dim(r_split, tm_idx, 0, keepdims=False)
    pieces = []
    for e in range(-(n_tm - 1), n_tm):
        if e == 0:
            pieces.append(own_piece)
            continue
        wanted = lax.dynamic_index_in_dim(r_split, jnp.clip(tm_idx - e, 0, n_tm - 1), 0, keepdims=False)
        pieces.append(passed_along(wanted, "tm", -e))
    relative = jnp.concatenate(pieces, axis=2)
    r16t = lax.dynamic_slice_in_dim(relative, (n_tm - 1 - tm_idx) * seg16, n_tm * seg16, 2)
    acc_rows = (pad + lags_span(all_lags, band) + pad) * chunk
    raw_half = pl.pallas_call(
        functools.partial(raw_kernel, lag_steps=lag_steps, rows=rows16, chunk=chunk, pad=pad, lags=all_lags),
        grid=(half,),
        in_specs=[
            pl.BlockSpec((1, band * chunk, rows16), lambda b: (b, 0, 0)),
            pl.BlockSpec((1, rows16 + lag_steps - 1, band * width), lambda b: (b, 0, 0)),
        ],
        out_specs=pl.BlockSpec((1, all_lags * chunk, width), lambda b: (b, 0, 0)),
        out_shape=jax.ShapeDtypeStruct((half, all_lags * chunk, width), jnp.float32),
        scratch_shapes=[pltpu.VMEM((acc_rows, 2 * width), jnp.float32)],
        interpret=_INTERPRET,
    )(r16t, m16)
    raw_half = raw_half.reshape(half, all_lags, chunk * width)
    own_raw = lax.all_to_all(raw_half, "sub", 1, 0, tiled=True)

    summed_dx = lax.psum_scatter(partial_dx, "sub", scatter_dimension=1, tiled=True)
    share4 = summed_dx.shape[1]
    own_steps = (
        seg_start
        + sub * share4 * tr
        + tr * jnp.arange(share4, dtype=jnp.int32)[:, None]
        + jnp.arange(tr, dtype=jnp.int32)[None, :]
    )
    dx = jnp.where(
        (own_steps >= fault_step[0])[None, :, :, None],
        summed_dx.reshape(nb, share4, tr, width),
        0.0,
    ).astype(jnp.bfloat16)
    voltage_grad = jnp.transpose(dx, (1, 2, 0, 3)).reshape(share4 * tr, nb * width)

    own_grad = own_raw
    own_squares = jnp.sum(own_grad * own_grad)
    total_squares = lax.psum(lax.psum(own_squares, ("bundle", "sub")), "tm")
    norm_limit = norm_ratio * math.sqrt(NB * L * CB * CB)
    factor = norm_limit / jnp.sqrt(total_squares + 1e-06)
    return (voltage_grad, own_grad * factor)


def solution(mesh):
    placed = (
        P(("case", "tm"), "bundle"),
        P(("case", "tm"), "bundle"),
        P("bundle", "sub", None),
        P("bundle", None),
        P("case"),
    )
    return jax.shard_map(
        local_body,
        mesh=mesh,
        in_specs=placed,
        out_specs=(P(("case", "tm", "sub"), "bundle"), P(("case", "bundle"), "sub", "tm")),
        check_vma=False,
    )
```
